768 devices in a mesh: ctx: 96 (over y, z), section: 2 (over core), tp: 4 (over x).
Axes of the slice: x: 4, y: 8, z: 12, core: 2. Of those that a mesh axis runs over, the one named last changes fastest.
Arguments:
- residual: bfloat16 [24576, 3584], P('ctx', 'tp'), may hold values from -6 to 6
- queries: bfloat16 [2, 24576, 2048], P('section', 'ctx', 'tp'), may hold values from -5 to 5
- keys: bfloat16 [2, 24576, 512], P('section', 'ctx', 'tp'), may hold values from -5 to 5
- window_values: bfloat16 [24576, 512], P('ctx', 'tp'), may hold values from -6 to 6
- mixing: bfloat16 [2, 2048, 3584], P('section', 'tp'), may hold values from -0.125 to 0.125
- norm_gain: bfloat16 [3584], replicated, may hold values from 0.5 to 1.5
- log_decay: float32 [24576, 16], P('ctx', 'tp'), may hold values from -1 to 0
- spike_counts: int32 [24576, 2048], P('ctx', 'tp'), may hold values from 0 to 3
- thresholds: float32 [2048], P('tp'), may hold values from 0.5 to 2
- lengths: int32 [96], replicated, may hold values from 128 to 256, as said below
Outputs:
- head_outputs: bfloat16 [2, 24576, 2048], P('section', 'ctx', 'tp')
- hidden: bfloat16 [24576, 3584], P('ctx', 'tp')
The draws below stay inside these ranges and needn't reach their ends.
Inputs may be any that keep to these rules, and one draw needn't show every extreme that they name: `lengths`: the valid tokens of a shard come first; some shard is full in every draw.
All inputs are finite; a program needn't handle non-finite values.
Results may differ from the reference program's by a relative error of at most 0.015.
Values may be sent and summed in bfloat16 or wider, within the bound.
No kernel may reach another device: no remote copies, remote signals or barrier semaphores. Data moves between devices by JAX's collectives and lax.ppermute only.
A program may use at most 128 MiB of HBM per device.

```python
import math
import jax
import jax.numpy as jnp
from jax import lax

D = 3584
KV_HEADS = 4
PROBE_BANDS = 16
HEAD = 128
WINDOW = 4096
TOK_DEV = 256
CONTEXT_EXTENT = 24576
SHARDS = 96
SECTIONS = 2
N_TP = 4


def draw_queries(key, part):
    shape = (SECTIONS, CONTEXT_EXTENT, PROBE_BANDS * HEAD)
    entries = jnp.clip(jax.random.normal(jax.random.fold_in(key, 1), shape, jnp.float32), -5.0, 5.0)
    return entries.astype(jnp.bfloat16)


def draw_keys(key, part):
    shape = (SECTIONS, CONTEXT_EXTENT, KV_HEADS * HEAD)
    entries = jnp.clip(jax.random.normal(jax.random.fold_in(key, 2), shape, jnp.float32), -5.0, 5.0)
    return entries.astype(jnp.bfloat16)


def draw_log_decay(key, part):
    slow_rate = -math.log(10.0) / CONTEXT_EXTENT * jax.random.uniform(jax.random.fold_in(key, 21), (PROBE_BANDS,), jnp.float32, 0.3, 1.0)
    fast_rate = -1.0 / jax.random.uniform(jax.random.fold_in(key, 22), (PROBE_BANDS,), jnp.float32, 30.0, 50.0)
    fast_share = 0.5
    picked = jax.random.uniform(jax.random.fold_in(key, 23), (PROBE_BANDS,)) < fast_share
    threshold_mark = jnp.where(picked, fast_rate, slow_rate)
    jitter_bias = jnp.exp(jax.random.uniform(jax.random.fold_in(key, 24), (CONTEXT_EXTENT, PROBE_BANDS), jnp.float32, -0.7, 0.7))
    pulse_train = jax.random.uniform(jax.random.fold_in(key, 25), (CONTEXT_EXTENT, PROBE_BANDS)) < 4.0 / CONTEXT_EXTENT
    pulse_train_height = jnp.log(jax.random.uniform(jax.random.fold_in(key, 26), (CONTEXT_EXTENT, PROBE_BANDS), jnp.float32, 0.5, 0.8))
    return jnp.where(pulse_train, pulse_train_height, threshold_mark[None, :] * jitter_bias).astype(jnp.float32)


def draw_lengths(key, part):
    drawn = jax.random.randint(jax.random.fold_in(key, 3), (SHARDS,), TOK_DEV // 2, TOK_DEV + 1)
    chosen = jax.random.randint(jax.random.fold_in(key, 4), (), 0, SHARDS)
    return jnp.where(jnp.arange(SHARDS) == chosen, TOK_DEV, drawn).astype(jnp.int32)


def place_ends(array, stream_key, least, top_value):
    extent = array.shape
    spot = [jax.random.randint(jax.random.fold_in(stream_key, axis), (), 0, extent[axis]) for axis in range(len(extent))]
    array = array.at[tuple(spot)].set(least)
    longest = extent.index(max(extent))
    spot[longest] = (spot[longest] + 1) % extent[longest]
    return array.at[tuple(spot)].set(top_value)


def levels(rng, extent, shards, least, top_value):
    def one(dim, shards_of):
        steps = jax.random.uniform(jax.random.fold_in(jax.random.fold_in(rng, 6), dim), (shards_of,), jnp.float32, least / len(shards), top_value / len(shards))
        return jnp.repeat(jnp.exp(steps), extent[dim] // shards_of).reshape((-1,) + (1,) * (len(extent) - dim - 1))

    gain = one(*shards[0])
    for cut in shards[1:]:
        gain = gain * one(*cut)
    return gain


def noise(key, shape, scale, most, shards=(), kind=jnp.bfloat16):
    factor_of = levels(key, shape, shards, -0.22, 0.18) if shards else 1.0
    values = jax.random.normal(key, shape, jnp.float32) * scale * factor_of
    return jnp.minimum(jnp.maximum(values, -most), most).astype(kind)


def setup_inputs(seed: int = 0) -> dict:
    seeds = jax.random.split(jax.random.key(seed), 11)
    return {
        "residual": noise(seeds[0], (CONTEXT_EXTENT, D), 1.0, 6.0, ((0, 96), (1, 4))),
        "queries": draw_queries(jax.random.fold_in(seeds[10], 71), 0),
        "keys": draw_keys(jax.random.fold_in(seeds[10], 71), 0),
        "window_values": noise(seeds[3], (CONTEXT_EXTENT, KV_HEADS * HEAD), 1.0, 6.0, ((0, 96), (1, 4))),
        "mixing": noise(seeds[4], (SECTIONS, PROBE_BANDS * HEAD, D), (PROBE_BANDS * HEAD) ** -0.5, 0.125, ((0, 2), (1, 4))),
        "norm_gain": jnp.clip(1.0 + 0.1 * jax.random.normal(seeds[5], (D,), jnp.float32), 0.5, 1.5).astype(jnp.bfloat16),
        "log_decay": draw_log_decay(jax.random.fold_in(seeds[10], 71), 0),
        "spike_counts": place_ends(jax.random.randint(seeds[7], (CONTEXT_EXTENT, PROBE_BANDS * HEAD), 0, 4), jax.random.fold_in(seeds[7], 1), 0, 3).astype(jnp.int32),
        "thresholds": jnp.clip(jnp.exp(math.log(2.0) - 1.3862944 * jax.random.uniform(seeds[8], (PROBE_BANDS * HEAD,), jnp.float32) ** levels(seeds[8], (PROBE_BANDS * HEAD,), ((0, 4),), -0.2, 0.2)), 0.5, 2.0),
        "lengths": draw_lengths(jax.random.fold_in(seeds[10], 71), 0),
    }


def reference(residual, queries, keys, window_values, mixing, norm_gain, log_decay, spike_counts, thresholds, lengths):
    group_size = PROBE_BANDS // KV_HEADS
    key_width = KV_HEADS * HEAD
    positions = jnp.arange(CONTEXT_EXTENT, dtype=jnp.int32)
    valid_rows = positions % TOK_DEV < lengths[positions // TOK_DEV]
    scale = 1.0 / math.sqrt(HEAD)
    padded_keys = jnp.concatenate([jnp.zeros((WINDOW, key_width), jnp.bfloat16), keys[0]], 0)
    padded_values = jnp.concatenate([jnp.zeros((WINDOW, key_width), jnp.bfloat16), window_values], 0)
    padded_valid = jnp.concatenate([jnp.arange(WINDOW, dtype=jnp.int32) < 0, valid_rows], 0)

    def window_block(block_index):
        start = (block_index * TOK_DEV).astype(jnp.int32)
        query_rows = lax.dynamic_slice_in_dim(queries[0], start, TOK_DEV, 0).astype(jnp.float32).reshape(TOK_DEV, KV_HEADS, group_size, HEAD)
        key_rows = lax.dynamic_slice_in_dim(padded_keys, start, WINDOW + TOK_DEV, 0).astype(jnp.float32).reshape(WINDOW + TOK_DEV, KV_HEADS, HEAD)
        value_rows = lax.dynamic_slice_in_dim(padded_values, start, WINDOW + TOK_DEV, 0).astype(jnp.float32).reshape(WINDOW + TOK_DEV, KV_HEADS, HEAD)
        key_valid = lax.dynamic_slice_in_dim(padded_valid, start, WINDOW + TOK_DEV, 0)
        scores = jnp.einsum('rgjd,kgd->gjrk', query_rows, key_rows) * scale
        distance = jnp.arange(TOK_DEV, dtype=jnp.int32)[:, None] + WINDOW - jnp.arange(WINDOW + TOK_DEV, dtype=jnp.int32)[None, :]
        allowed = key_valid[None, :] & (distance >= 0) & (distance < WINDOW)
        masked = jnp.where(allowed, scores, -1e+30)
        highest = lax.optimization_barrier(jnp.max(masked, axis=-1, keepdims=True))
        weights = jnp.where(allowed, jnp.exp(masked - highest), 0.0)
        totals = jnp.maximum(lax.optimization_barrier(jnp.sum(weights, axis=-1)), 1.0)
        rounded = lax.optimization_barrier(weights.astype(jnp.bfloat16)).astype(jnp.float32)
        blended = jnp.einsum('gjrk,kgd->gjrd', rounded, value_rows) / totals[..., None]
        blended = blended.transpose(2, 0, 1, 3).reshape(TOK_DEV, PROBE_BANDS * HEAD)
        row_valid = lax.dynamic_slice_in_dim(valid_rows, start, TOK_DEV, 0)
        return jnp.where(row_valid[:, None], blended, 0.0).astype(jnp.bfloat16)
    attention = lax.map(window_block, jnp.arange(SHARDS, dtype=jnp.int32)).reshape(CONTEXT_EXTENT, PROBE_BANDS * HEAD)
    width = PROBE_BANDS * HEAD // N_TP
    summed = residual.astype(jnp.float32)
    for member in range(N_TP):
        term = jnp.dot(attention[:, member * width:(member + 1) * width], mixing[0, member * width:(member + 1) * width], preferred_element_type=jnp.float32)
        summed = summed + lax.optimization_barrier(term.astype(jnp.bfloat16)).astype(jnp.float32)
    hidden = summed.astype(jnp.bfloat16)
    wide = hidden.astype(jnp.float32)
    normed = (wide * lax.rsqrt(lax.optimization_barrier(jnp.mean(wide * wide, axis=-1, keepdims=True)) + 1e-05) * norm_gain.astype(jnp.float32)).astype(jnp.bfloat16)
    payload_vectors = lax.dot_general(normed, mixing[1], (((1,), (1,)), ((), ())), preferred_element_type=jnp.float32).astype(jnp.bfloat16)
    decay_all = log_decay * valid_rows[:, None].astype(jnp.float32)
    masked_keys = jnp.where(valid_rows[:, None], keys[1], jnp.zeros_like(keys[1]))
    triangle = jnp.arange(TOK_DEV, dtype=jnp.int32)[:, None] >= jnp.arange(TOK_DEV, dtype=jnp.int32)[None, :]

    def linear_block(state, block_index):
        start = (block_index * TOK_DEV).astype(jnp.int32)
        query_rows = lax.dynamic_slice_in_dim(queries[1], start, TOK_DEV, 0).astype(jnp.float32).reshape(TOK_DEV, KV_HEADS, group_size, HEAD)
        key_rows = lax.dynamic_slice_in_dim(masked_keys, start, TOK_DEV, 0).astype(jnp.float32).reshape(TOK_DEV, KV_HEADS, HEAD)
        value_rows = lax.dynamic_slice_in_dim(payload_vectors, start, TOK_DEV, 0).astype(jnp.float32).reshape(TOK_DEV, KV_HEADS, group_size, HEAD)
        decays = lax.dynamic_slice_in_dim(decay_all, start, TOK_DEV, 0).reshape(TOK_DEV, KV_HEADS, group_size)
        cumulated = jnp.cumsum(decays, axis=0)
        block_total = cumulated[-1]
        inter = jnp.einsum('rgjd,gdje->rgje', query_rows, state, precision=lax.Precision.HIGHEST) * jnp.exp(cumulated)[..., None]
        products = jnp.einsum('rgjd,sgd->gjrs', query_rows, key_rows)
        ordered = cumulated.transpose(1, 2, 0)
        spread = ordered[..., :, None] - ordered[..., None, :]
        damping = jnp.where(triangle, jnp.exp(jnp.minimum(spread, 0.0)), 0.0)
        intra = jnp.einsum('gjrs,sgje->rgje', products * damping, value_rows, precision=lax.Precision.HIGHEST)
        fresh_state = jnp.einsum('sgd,sgje->gdje', key_rows, value_rows * jnp.exp(block_total - cumulated)[..., None], precision=lax.Precision.HIGHEST)
        state = state * jnp.exp(block_total)[:, None, :, None] + fresh_state
        return (state, inter + intra)
    start_state = jnp.zeros((KV_HEADS, HEAD, group_size, HEAD), jnp.float32)
    unused_state, linear_rows = lax.scan(linear_block, start_state, jnp.arange(SHARDS, dtype=jnp.int32))
    mixed = linear_rows.reshape(CONTEXT_EXTENT, PROBE_BANDS, HEAD)
    scaled = mixed * lax.rsqrt(lax.optimization_barrier(jnp.mean(mixed * mixed, axis=-1, keepdims=True)) + 1e-05)
    gating = spike_counts.astype(jnp.float32).reshape(CONTEXT_EXTENT, PROBE_BANDS, HEAD) * thresholds.reshape(PROBE_BANDS, HEAD)
    gated = jnp.where(valid_rows[:, None], (scaled * gating).reshape(CONTEXT_EXTENT, PROBE_BANDS * HEAD), 0.0).astype(jnp.bfloat16)
    return (jnp.stack([attention, gated], 0), hidden)
```

```python
import math

import jax
import jax.numpy as jnp
from jax import lax
from jax.sharding import PartitionSpec as P

HEAD = 128
WINDOW = 4096


def passed_along(x, by, section):
    shards = lax.axis_size("ctx")
    sections = lax.axis_size("section")
    pairs = [
        (i * sections + section, (i + by) * sections + section)
        for i in range(shards)
        if 0 <= i + by < shards
    ]
    return lax.ppermute(x, ("ctx", "section"), pairs)


def body(
    residual,
    queries,
    keys,
    window_values,
    mixing,
    norm_gain,
    log_decay,
    spike_counts,
    thresholds,
    lengths,
):
    section_index = lax.axis_index("section")
    shard_index = lax.axis_index("ctx")
    shards = lax.axis_size("ctx")
    row_count = keys.shape[1]
    head_size = HEAD
    key_heads = keys.shape[2] // head_size
    query_head_rows = queries.shape[2] // head_size
    group_size = query_head_rows // key_heads
    span_blocks = WINDOW // row_count
    feature_count = mixing.shape[2]
    scale = 1.0 / math.sqrt(head_size)
    positions = jnp.arange(row_count, dtype=jnp.int32)
    valid_rows = positions < lengths[shard_index]
    own_keys = keys[0]

    query_rows = queries[0].reshape(row_count, key_heads, group_size, head_size)
    base_distance = positions[:, None] - positions[None, :]
    running = jnp.zeros((key_heads, group_size, row_count, head_size), jnp.float32)
    totals = jnp.zeros((key_heads, group_size, row_count), jnp.float32)
    best = jnp.full((key_heads, group_size, row_count), -1e30, jnp.float32)
    for distance_blocks in range(span_blocks + 1):
        if distance_blocks == 0:
            key_block, value_block = own_keys, window_values
        else:
            key_block, value_block = passed_along(
                (own_keys, window_values), distance_blocks, 0
            )
        source = shard_index - distance_blocks
        key_valid = (source >= 0) & (positions < lengths[jnp.maximum(source, 0)])
        scores = (
            jnp.einsum(
                "rgjd,kgd->gjrk",
                query_rows,
                key_block.reshape(row_count, key_heads, head_size),
                preferred_element_type=jnp.float32,
            )
            * scale
        )
        distance = base_distance + distance_blocks * row_count
        allowed = key_valid[None, :] & (distance >= 0) & (distance < WINDOW)
        scores = jnp.where(allowed, scores, -1e30)
        new_best = jnp.maximum(best, jnp.max(scores, axis=-1))
        factor = jnp.exp(best - new_best)
        weights = jnp.where(allowed, jnp.exp(scores - new_best[..., None]), 0.0)
        blended = jnp.einsum(
            "gjrk,kgd->gjrd",
            weights.astype(jnp.bfloat16),
            value_block.reshape(row_count, key_heads, head_size),
            preferred_element_type=jnp.float32,
        )
        running = running * factor[..., None] + blended
        totals = totals * factor + jnp.sum(weights, axis=-1)
        best = new_best
    attention = running / jnp.maximum(totals, 1.0)[..., None]
    attention = attention.transpose(2, 0, 1, 3).reshape(row_count, query_head_rows * head_size)
    attention = jnp.where(valid_rows[:, None], attention, 0.0).astype(jnp.bfloat16)
    projected = jnp.dot(attention, mixing[0], preferred_element_type=jnp.float32)

    share = lax.psum_scatter(
        projected.astype(jnp.bfloat16), "tp", scatter_dimension=1, tiled=True
    ).astype(jnp.float32)
    own_hidden = (share + residual.astype(jnp.float32)).astype(jnp.bfloat16)
    moved_share = lax.ppermute(own_hidden, "section", [(0, 1)])
    local_activations = jnp.where(section_index == 0, own_hidden, moved_share)
    complete_hidden_matrix = lax.all_gather(local_activations, "tp", axis=1, tiled=True)

    masked_keys = jnp.where(valid_rows[:, None], own_keys, jnp.zeros_like(own_keys)).reshape(
        row_count, key_heads, head_size
    )
    wide_keys = masked_keys.astype(jnp.float32)
    decays = log_decay * valid_rows[:, None].astype(jnp.float32)
    wide = complete_hidden_matrix.astype(jnp.float32)
    normed = (
        wide
        * lax.rsqrt(jnp.mean(wide * wide, axis=-1, keepdims=True) + 1e-05)
        * norm_gain.astype(jnp.float32)
    ).astype(jnp.bfloat16)
    payload_vectors = lax.dot_general(
        normed, mixing[0], (((1,), (1,)), ((), ())), preferred_element_type=jnp.float32
    ).astype(jnp.bfloat16)
    cumulated = jnp.cumsum(decays, axis=0).reshape(row_count, key_heads, group_size)
    value_rows = payload_vectors.astype(jnp.float32).reshape(
        row_count, key_heads, group_size, head_size
    )
    fresh_state = jnp.einsum(
        "sgd,sgje->gdje",
        wide_keys,
        value_rows * jnp.exp(cumulated[-1] - cumulated)[..., None],
        precision=lax.Precision.HIGHEST,
    )

    def chain(previous_entry, latter):
        return (
            previous_entry[0] + latter[0],
            previous_entry[1] * jnp.exp(latter[0])[:, None, :, None] + latter[1],
        )

    entry = passed_along((cumulated[-1], fresh_state), 1, 1)
    reach = 1
    while reach < shards:
        entry = chain(passed_along(entry, reach, 1), entry)
        reach *= 2
    incoming = entry[1]

    query_narrow = queries[0].reshape(row_count, key_heads, group_size, head_size)
    query_wide = query_narrow.astype(jnp.float32)
    products = jnp.einsum(
        "rgjd,sgd->gjrs", query_narrow, masked_keys, preferred_element_type=jnp.float32
    )
    ordered = cumulated.transpose(1, 2, 0)
    spread = ordered[..., :, None] - ordered[..., None, :]
    triangle = positions[:, None] >= positions[None, :]
    damping = jnp.where(triangle, jnp.exp(jnp.minimum(spread, 0.0)), 0.0)
    intra = jnp.einsum(
        "gjrs,sgje->rgje", products * damping, value_rows, precision=lax.Precision.HIGHEST
    )
    inter = (
        jnp.einsum("rgjd,gdje->rgje", query_wide, incoming, precision=lax.Precision.HIGHEST)
        * jnp.exp(cumulated)[..., None]
    )
    mixed = (inter + intra).reshape(row_count, query_head_rows, head_size)
    scaled = mixed * lax.rsqrt(jnp.mean(mixed * mixed, axis=-1, keepdims=True) + 1e-05)
    gating = spike_counts.astype(jnp.float32).reshape(
        row_count, query_head_rows, head_size
    ) * thresholds.reshape(query_head_rows, head_size)
    gated = jnp.where(
        valid_rows[:, None],
        (scaled * gating).reshape(row_count, query_head_rows * head_size),
        0.0,
    ).astype(jnp.bfloat16)
    head_outputs = jnp.where(section_index == 0, attention, gated)[None]
    return (head_outputs, local_activations)


def solution(mesh):
    return jax.shard_map(
        body,
        mesh=mesh,
        in_specs=(
            P("ctx", "tp"),
            P("section", "ctx", "tp"),
            P("section", "ctx", "tp"),
            P("ctx", "tp"),
            P("section", "tp", None),
            P(),
            P("ctx", "tp"),
            P("ctx", "tp"),
            P("tp"),
            P(),
        ),
        out_specs=(P("section", "ctx", "tp"), P("ctx", "tp")),
        check_vma=False,
    )
```

```python
import math

import jax
import jax.numpy as jnp
from jax import lax
from jax.sharding import PartitionSpec as P

HEAD = 128
WINDOW = 4096


def passed_along(x, by, section):
    shards = lax.axis_size("ctx")
    sections = lax.axis_size("section")
    pairs = [
        (i * sections + section, (i + by) * sections + section)
        for i in range(shards)
        if 0 <= i + by < shards
    ]
    return lax.ppermute(x, ("ctx", "section"), pairs)


def body(
    residual,
    queries,
    keys,
    window_values,
    mixing,
    norm_gain,
    log_decay,
    spike_counts,
    thresholds,
    lengths,
):
    section_index = lax.axis_index("section")
    shard_index = lax.axis_index("ctx")
    shards = lax.axis_size("ctx")
    row_count = keys.shape[1]
    head_size = HEAD
    key_heads = keys.shape[2] // head_size
    query_head_rows = queries.shape[2] // head_size
    group_size = query_head_rows // key_heads
    span_blocks = WINDOW // row_count
    feature_count = mixing.shape[2]
    scale = 1.0 / math.sqrt(head_size)
    positions = jnp.arange(row_count, dtype=jnp.int32)
    valid_rows = positions < lengths[shard_index]
    own_keys = keys[0]

    query_rows = queries[0].reshape(row_count, key_heads, group_size, head_size)
    base_distance = positions[:, None] - positions[None, :]
    key_width = own_keys.shape[1]
    packed = jnp.concatenate([own_keys, window_values], axis=1)
    running = jnp.zeros((key_heads, group_size, row_count, head_size), jnp.float32)
    totals = jnp.zeros((key_heads, group_size, row_count), jnp.float32)
    best = jnp.full((key_heads, group_size, row_count), -1e30, jnp.float32)
    for distance_blocks in range(span_blocks + 1):
        if distance_blocks == 0:
            key_block, value_block = own_keys, window_values
        else:
            joined = passed_along(packed, distance_blocks, 0)
            key_block, value_block = joined[:, :key_width], joined[:, key_width:]
        source = shard_index - distance_blocks
        key_valid = (source >= 0) & (positions < lengths[jnp.maximum(source, 0)])
        scores = (
            jnp.einsum(
                "rgjd,kgd->gjrk",
                query_rows,
                key_block.reshape(row_count, key_heads, head_size),
                preferred_element_type=jnp.float32,
            )
            * scale
        )
        distance = base_distance + distance_blocks * row_count
        allowed = key_valid[None, :] & (distance >= 0) & (distance < WINDOW)
        scores = jnp.where(allowed, scores, -1e30)
        new_best = jnp.maximum(best, jnp.max(scores, axis=-1))
        factor = jnp.exp(best - new_best)
        weights = jnp.where(allowed, jnp.exp(scores - new_best[..., None]), 0.0)
        blended = jnp.einsum(
            "gjrk,kgd->gjrd",
            weights.astype(jnp.bfloat16),
            value_block.reshape(row_count, key_heads, head_size),
            preferred_element_type=jnp.float32,
        )
        running = running * factor[..., None] + blended
        totals = totals * factor + jnp.sum(weights, axis=-1)
        best = new_best
    attention = running / jnp.maximum(totals, 1.0)[..., None]
    attention = attention.transpose(2, 0, 1, 3).reshape(row_count, query_head_rows * head_size)
    attention = jnp.where(valid_rows[:, None], attention, 0.0).astype(jnp.bfloat16)
    projected = jnp.dot(attention, mixing[0], preferred_element_type=jnp.float32)

    members = lax.axis_size("tp")
    member = lax.axis_index("tp")
    width = feature_count // members
    terms = projected.astype(jnp.bfloat16)
    summed = residual.astype(jnp.float32) + lax.dynamic_slice_in_dim(
        terms, member * width, width, 1
    ).astype(jnp.float32)
    for step in range(1, members):
        target = (member + step) % members
        sent = lax.dynamic_slice_in_dim(terms, target * width, width, 1)
        pairs = [(m, (m + step) % members) for m in range(members)]
        summed = summed + lax.ppermute(sent, ("section", "tp"), pairs).astype(jnp.float32)
    own_hidden = summed.astype(jnp.bfloat16)
    arrived = jnp.stack(
        [
            lax.ppermute(
                own_hidden,
                ("section", "tp"),
                [(m, members + (m + step) % members) for m in range(members)],
            )
            for step in range(members)
        ],
        0,
    )
    local_activations = jnp.where(section_index == 0, own_hidden, arrived[0])
    order = (member - jnp.arange(members, dtype=jnp.int32)) % members
    complete_hidden_matrix = (
        jnp.take(arrived, order, axis=0).transpose(1, 0, 2).reshape(row_count, feature_count)
    )

    masked_keys = jnp.where(valid_rows[:, None], own_keys, jnp.zeros_like(own_keys)).reshape(
        row_count, key_heads, head_size
    )
    wide_keys = masked_keys.astype(jnp.float32)
    decays = log_decay * valid_rows[:, None].astype(jnp.float32)
    wide = complete_hidden_matrix.astype(jnp.float32)
    normed = (
        wide
        * lax.rsqrt(jnp.mean(wide * wide, axis=-1, keepdims=True) + 1e-05)
        * norm_gain.astype(jnp.float32)
    ).astype(jnp.bfloat16)
    payload_vectors = lax.dot_general(
        normed, mixing[0], (((1,), (1,)), ((), ())), preferred_element_type=jnp.float32
    ).astype(jnp.bfloat16)
    cumulated = jnp.cumsum(decays, axis=0).reshape(row_count, key_heads, group_size)
    value_rows = payload_vectors.astype(jnp.float32).reshape(
        row_count, key_heads, group_size, head_size
    )
    fresh_state = jnp.einsum(
        "sgd,sgje->gdje",
        wide_keys,
        value_rows * jnp.exp(cumulated[-1] - cumulated)[..., None],
        precision=lax.Precision.HIGHEST,
    )

    def chain(previous_entry, latter):
        latter_total = latter[:, :1]
        return jnp.concatenate(
            [
                previous_entry[:, :1] + latter_total,
                previous_entry[:, 1:] * jnp.exp(latter_total) + latter[:, 1:],
            ],
            axis=1,
        )

    total_rows = jnp.broadcast_to(cumulated[-1][:, None, :, None], (key_heads, 1, group_size, head_size))
    entry = passed_along(jnp.concatenate([total_rows, fresh_state], axis=1), 1, 1)
    reach = 1
    while reach < shards:
        entry = chain(passed_along(entry, reach, 1), entry)
        reach *= 2
    incoming = entry[:, 1:]

    query_narrow = queries[0].reshape(row_count, key_heads, group_size, head_size)
    query_wide = query_narrow.astype(jnp.float32)
    products = jnp.einsum(
        "rgjd,sgd->gjrs", query_narrow, masked_keys, preferred_element_type=jnp.float32
    )
    ordered = cumulated.transpose(1, 2, 0)
    spread = ordered[..., :, None] - ordered[..., None, :]
    triangle = positions[:, None] >= positions[None, :]
    damping = jnp.where(triangle, jnp.exp(jnp.minimum(spread, 0.0)), 0.0)
    intra = jnp.einsum(
        "gjrs,sgje->rgje", products * damping, value_rows, precision=lax.Precision.HIGHEST
    )
    inter = (
        jnp.einsum("rgjd,gdje->rgje", query_wide, incoming, precision=lax.Precision.HIGHEST)
        * jnp.exp(cumulated)[..., None]
    )
    mixed = (inter + intra).reshape(row_count, query_head_rows, head_size)
    scaled = mixed * lax.rsqrt(jnp.mean(mixed * mixed, axis=-1, keepdims=True) + 1e-05)
    gating = spike_counts.astype(jnp.float32).reshape(
        row_count, query_head_rows, head_size
    ) * thresholds.reshape(query_head_rows, head_size)
    gated = jnp.where(
        valid_rows[:, None],
        (scaled * gating).reshape(row_count, query_head_rows * head_size),
        0.0,
    ).astype(jnp.bfloat16)
    head_outputs = jnp.where(section_index == 0, attention, gated)[None]
    return (head_outputs, local_activations)


def solution(mesh):
    return jax.shard_map(
        body,
        mesh=mesh,
        in_specs=(
            P("ctx", "tp"),
            P("section", "ctx", "tp"),
            P("section", "ctx", "tp"),
            P("ctx", "tp"),
            P("section", "tp", None),
            P(),
            P("ctx", "tp"),
            P("ctx", "tp"),
            P("tp"),
            P(),
        ),
        out_specs=(P("section", "ctx", "tp"), P("ctx", "tp")),
        check_vma=False,
    )
```

```python
import math

import jax
import jax.numpy as jnp
from jax import lax
from jax.sharding import PartitionSpec as P

HEAD = 128
WINDOW = 4096


def passed_along(x, by, section):
    shards = lax.axis_size("ctx")
    sections = lax.axis_size("section")
    pairs = [
        (i * sections + section, (i + by) * sections + section)
        for i in range(shards)
        if 0 <= i + by < shards
    ]
    return lax.ppermute(x, ("ctx", "section"), pairs)


def body(
    residual,
    queries,
    keys,
    window_values,
    mixing,
    norm_gain,
    log_decay,
    spike_counts,
    thresholds,
    lengths,
):
    section_index = lax.axis_index("section")
    shard_index = lax.axis_index("ctx")
    shards = lax.axis_size("ctx")
    row_count = keys.shape[1]
    head_size = HEAD
    key_heads = keys.shape[2] // head_size
    query_head_rows = queries.shape[2] // head_size
    group_size = query_head_rows // key_heads
    span_blocks = WINDOW // row_count
    feature_count = mixing.shape[2]
    scale = 1.0 / math.sqrt(head_size)
    positions = jnp.arange(row_count, dtype=jnp.int32)
    valid_rows = positions < lengths[shard_index]
    own_keys = keys[0]

    query_rows = queries[0].reshape(row_count, key_heads, group_size, head_size)
    base_distance = positions[:, None] - positions[None, :]
    key_width = own_keys.shape[1]
    packed = jnp.concatenate([own_keys, window_values], axis=1)
    running = jnp.zeros((key_heads, group_size, row_count, head_size), jnp.float32)
    totals = jnp.zeros((key_heads, group_size, row_count), jnp.float32)
    best = jnp.full((key_heads, group_size, row_count), -1e30, jnp.float32)
    for distance_blocks in range(span_blocks + 1):
        if distance_blocks == 0:
            key_block, value_block = own_keys, window_values
        else:
            joined = passed_along(packed, distance_blocks, 0)
            key_block, value_block = joined[:, :key_width], joined[:, key_width:]
        source = shard_index - distance_blocks
        key_valid = (source >= 0) & (positions < lengths[jnp.maximum(source, 0)])
        scores = (
            jnp.einsum(
                "rgjd,kgd->gjrk",
                query_rows,
                key_block.reshape(row_count, key_heads, head_size),
                preferred_element_type=jnp.float32,
            )
            * scale
        )
        distance = base_distance + distance_blocks * row_count
        allowed = key_valid[None, :] & (distance >= 0) & (distance < WINDOW)
        scores = jnp.where(allowed, scores, -1e30)
        new_best = jnp.maximum(best, jnp.max(scores, axis=-1))
        factor = jnp.exp(best - new_best)
        weights = jnp.where(allowed, jnp.exp(scores - new_best[..., None]), 0.0)
        blended = jnp.einsum(
            "gjrk,kgd->gjrd",
            weights.astype(jnp.bfloat16),
            value_block.reshape(row_count, key_heads, head_size),
            preferred_element_type=jnp.float32,
        )
        running = running * factor[..., None] + blended
        totals = totals * factor + jnp.sum(weights, axis=-1)
        best = new_best
    attention = running / jnp.maximum(totals, 1.0)[..., None]
    attention = attention.transpose(2, 0, 1, 3).reshape(row_count, query_head_rows * head_size)
    attention = jnp.where(valid_rows[:, None], attention, 0.0).astype(jnp.bfloat16)
    projected = jnp.dot(attention, mixing[0], preferred_element_type=jnp.float32)

    members = lax.axis_size("tp")
    member = lax.axis_index("tp")
    width = feature_count // members
    terms = projected.astype(jnp.bfloat16)
    summed = residual.astype(jnp.float32) + lax.dynamic_slice_in_dim(
        terms, member * width, width, 1
    ).astype(jnp.float32)
    for step in range(1, members):
        target = (member + step) % members
        sent = lax.dynamic_slice_in_dim(terms, target * width, width, 1)
        pairs = [(m, (m + step) % members) for m in range(members)]
        summed = summed + lax.ppermute(sent, ("section", "tp"), pairs).astype(jnp.float32)
    own_hidden = summed.astype(jnp.bfloat16)
    arrived = jnp.stack(
        [
            lax.ppermute(
                own_hidden,
                ("section", "tp"),
                [(m, members + (m + step) % members) for m in range(members)],
            )
            for step in range(members)
        ],
        0,
    )
    local_activations = jnp.where(section_index == 0, own_hidden, arrived[0])
    order = (member - jnp.arange(members, dtype=jnp.int32)) % members
    complete_hidden_matrix = (
        jnp.take(arrived, order, axis=0).transpose(1, 0, 2).reshape(row_count, feature_count)
    )

    masked_keys = jnp.where(valid_rows[:, None], own_keys, jnp.zeros_like(own_keys)).reshape(
        row_count, key_heads, head_size
    )
    wide_keys = masked_keys.astype(jnp.float32)
    decays = log_decay * valid_rows[:, None].astype(jnp.float32)
    wide = complete_hidden_matrix.astype(jnp.float32)
    normed = (
        wide
        * lax.rsqrt(jnp.mean(wide * wide, axis=-1, keepdims=True) + 1e-05)
        * norm_gain.astype(jnp.float32)
    ).astype(jnp.bfloat16)
    payload_vectors = lax.dot_general(
        normed, mixing[0], (((1,), (1,)), ((), ())), preferred_element_type=jnp.float32
    ).astype(jnp.bfloat16)
    cumulated = jnp.cumsum(decays, axis=0).reshape(row_count, key_heads, group_size)
    value_rows = payload_vectors.astype(jnp.float32).reshape(
        row_count, key_heads, group_size, head_size
    )
    fresh_state = jnp.einsum(
        "sgd,sgje->gdje",
        wide_keys,
        value_rows * jnp.exp(cumulated[-1] - cumulated)[..., None],
        precision=lax.Precision.HIGHEST,
    )

    def chain(previous_entry, latter):
        latter_total = latter[:, :1]
        return jnp.concatenate(
            [
                previous_entry[:, :1] + latter_total,
                previous_entry[:, 1:] * jnp.exp(latter_total) + latter[:, 1:],
            ],
            axis=1,
        )

    def sent_along(entry, by):
        total = entry[:, :1]
        high = total.astype(jnp.bfloat16)
        low = (total - high.astype(jnp.float32)).astype(jnp.bfloat16)
        narrow = jnp.concatenate([high, low, entry[:, 1:].astype(jnp.bfloat16)], axis=1)
        moved = passed_along(narrow, by, 1).astype(jnp.float32)
        return jnp.concatenate([moved[:, :1] + moved[:, 1:2], moved[:, 2:]], axis=1)

    total_rows = jnp.broadcast_to(cumulated[-1][:, None, :, None], (key_heads, 1, group_size, head_size))
    entry = sent_along(jnp.concatenate([total_rows, fresh_state], axis=1), 1)
    reach = 1
    while reach < shards:
        entry = chain(sent_along(entry, reach), entry)
        reach *= 2
    incoming = entry[:, 1:]

    query_narrow = queries[0].reshape(row_count, key_heads, group_size, head_size)
    query_wide = query_narrow.astype(jnp.float32)
    products = jnp.einsum(
        "rgjd,sgd->gjrs", query_narrow, masked_keys, preferred_element_type=jnp.float32
    )
    ordered = cumulated.transpose(1, 2, 0)
    spread = ordered[..., :, None] - ordered[..., None, :]
    triangle = positions[:, None] >= positions[None, :]
    damping = jnp.where(triangle, jnp.exp(jnp.minimum(spread, 0.0)), 0.0)
    intra = jnp.einsum(
        "gjrs,sgje->rgje", products * damping, value_rows, precision=lax.Precision.HIGHEST
    )
    inter = (
        jnp.einsum("rgjd,gdje->rgje", query_wide, incoming, precision=lax.Precision.HIGHEST)
        * jnp.exp(cumulated)[..., None]
    )
    mixed = (inter + intra).reshape(row_count, query_head_rows, head_size)
    scaled = mixed * lax.rsqrt(jnp.mean(mixed * mixed, axis=-1, keepdims=True) + 1e-05)
    gating = spike_counts.astype(jnp.float32).reshape(
        row_count, query_head_rows, head_size
    ) * thresholds.reshape(query_head_rows, head_size)
    gated = jnp.where(
        valid_rows[:, None],
        (scaled * gating).reshape(row_count, query_head_rows * head_size),
        0.0,
    ).astype(jnp.bfloat16)
    head_outputs = jnp.where(section_index == 0, attention, gated)[None]
    return (head_outputs, local_activations)


def solution(mesh):
    return jax.shard_map(
        body,
        mesh=mesh,
        in_specs=(
            P("ctx", "tp"),
            P("section", "ctx", "tp"),
            P("section", "ctx", "tp"),
            P("ctx", "tp"),
            P("section", "tp", None),
            P(),
            P("ctx", "tp"),
            P("ctx", "tp"),
            P("tp"),
            P(),
        ),
        out_specs=(P("section", "ctx", "tp"), P("ctx", "tp")),
        check_vma=False,
    )
```

```python
import math

import jax
import jax.numpy as jnp
from jax import lax
from jax.sharding import PartitionSpec as P

HEAD = 128
WINDOW = 4096


def passed_along(x, by, section):
    shards = lax.axis_size("ctx")
    sections = lax.axis_size("section")
    pairs = [
        (i * sections + section, (i + by) * sections + section)
        for i in range(shards)
        if 0 <= i + by < shards
    ]
    return lax.ppermute(x, ("ctx", "section"), pairs)


def body(
    residual,
    queries,
    keys,
    window_values,
    mixing,
    norm_gain,
    log_decay,
    spike_counts,
    thresholds,
    lengths,
):
    section_index = lax.axis_index("section")
    shard_index = lax.axis_index("ctx")
    shards = lax.axis_size("ctx")
    row_count = keys.shape[1]
    head_size = HEAD
    key_heads = keys.shape[2] // head_size
    query_head_rows = queries.shape[2] // head_size
    group_size = query_head_rows // key_heads
    span_blocks = WINDOW // row_count
    feature_count = mixing.shape[2]
    scale = 1.0 / math.sqrt(head_size)
    positions = jnp.arange(row_count, dtype=jnp.int32)
    valid_rows = positions < lengths[shard_index]
    own_keys = keys[0]

    query_rows = queries[0].reshape(row_count, key_heads, group_size, head_size)
    base_distance = positions[:, None] - positions[None, :]
    key_width = own_keys.shape[1]
    packed = jnp.concatenate([own_keys, window_values], axis=1)
    running = jnp.zeros((key_heads, group_size, row_count, head_size), jnp.float32)
    totals = jnp.zeros((key_heads, group_size, row_count), jnp.float32)
    best = jnp.full((key_heads, group_size, row_count), -1e30, jnp.float32)
    for distance_blocks in range(span_blocks + 1):
        if distance_blocks == 0:
            key_block, value_block = own_keys, window_values
        else:
            joined = passed_along(packed, distance_blocks, 0)
            key_block, value_block = joined[:, :key_width], joined[:, key_width:]
        source = shard_index - distance_blocks
        key_valid = (source >= 0) & (positions < lengths[jnp.maximum(source, 0)])
        scores = (
            jnp.einsum(
                "rgjd,kgd->gjrk",
                query_rows,
                key_block.reshape(row_count, key_heads, head_size),
                preferred_element_type=jnp.float32,
            )
            * scale
        )
        distance = base_distance + distance_blocks * row_count
        allowed = key_valid[None, :] & (distance >= 0) & (distance < WINDOW)
        scores = jnp.where(allowed, scores, -1e30)
        new_best = jnp.maximum(best, jnp.max(scores, axis=-1))
        factor = jnp.exp(best - new_best)
        weights = jnp.where(allowed, jnp.exp(scores - new_best[..., None]), 0.0)
        blended = jnp.einsum(
            "gjrk,kgd->gjrd",
            weights.astype(jnp.bfloat16),
            value_block.reshape(row_count, key_heads, head_size),
            preferred_element_type=jnp.float32,
        )
        running = running * factor[..., None] + blended
        totals = totals * factor + jnp.sum(weights, axis=-1)
        best = new_best
    attention = running / jnp.maximum(totals, 1.0)[..., None]
    attention = attention.transpose(2, 0, 1, 3).reshape(row_count, query_head_rows * head_size)
    attention = jnp.where(valid_rows[:, None], attention, 0.0).astype(jnp.bfloat16)
    projected = jnp.dot(attention, mixing[0], preferred_element_type=jnp.float32)

    members = lax.axis_size("tp")
    member = lax.axis_index("tp")
    width = feature_count // members
    terms = projected.astype(jnp.bfloat16)
    summed = residual.astype(jnp.float32) + lax.dynamic_slice_in_dim(
        terms, member * width, width, 1
    ).astype(jnp.float32)
    for step in range(1, members):
        target = (member + step) % members
        sent = lax.dynamic_slice_in_dim(terms, target * width, width, 1)
        pairs = [(m, (m + step) % members) for m in range(members)]
        summed = summed + lax.ppermute(sent, ("section", "tp"), pairs).astype(jnp.float32)
    own_hidden = summed.astype(jnp.bfloat16)
    arrived = jnp.stack(
        [
            lax.ppermute(
                own_hidden,
                ("section", "tp"),
                [(m, members + (m + step) % members) for m in range(members)],
            )
            for step in range(members)
        ],
        0,
    )
    local_activations = jnp.where(section_index == 0, own_hidden, arrived[0])
    order = (member - jnp.arange(members, dtype=jnp.int32)) % members
    complete_hidden_matrix = (
        jnp.take(arrived, order, axis=0).transpose(1, 0, 2).reshape(row_count, feature_count)
    )

    masked_keys = jnp.where(valid_rows[:, None], own_keys, jnp.zeros_like(own_keys)).reshape(
        row_count, key_heads, head_size
    )
    wide_keys = masked_keys.astype(jnp.float32)
    decays = log_decay * valid_rows[:, None].astype(jnp.float32)
    wide = complete_hidden_matrix.astype(jnp.float32)
    normed = (
        wide
        * lax.rsqrt(jnp.mean(wide * wide, axis=-1, keepdims=True) + 1e-05)
        * norm_gain.astype(jnp.float32)
    ).astype(jnp.bfloat16)
    payload_vectors = lax.dot_general(
        normed, mixing[0], (((1,), (1,)), ((), ())), preferred_element_type=jnp.float32
    ).astype(jnp.bfloat16)
    cumulated = jnp.cumsum(decays, axis=0).reshape(row_count, key_heads, group_size)
    value_rows = payload_vectors.astype(jnp.float32).reshape(
        row_count, key_heads, group_size, head_size
    )
    fresh_state = jnp.einsum(
        "sgd,sgje->gdje",
        wide_keys,
        value_rows * jnp.exp(cumulated[-1] - cumulated)[..., None],
        precision=lax.Precision.HIGHEST,
    )

    def chain(previous_entry, latter):
        latter_total = latter[:, :1]
        return jnp.concatenate(
            [
                previous_entry[:, :1] + latter_total,
                previous_entry[:, 1:] * jnp.exp(latter_total) + latter[:, 1:],
            ],
            axis=1,
        )

    def sent_along(entry, by):
        total = entry[:, :1]
        high = total.astype(jnp.bfloat16)
        low = (total - high.astype(jnp.float32)).astype(jnp.bfloat16)
        narrow = jnp.concatenate([high, low, entry[:, 1:].astype(jnp.bfloat16)], axis=1)
        moved = passed_along(narrow, by, 1).astype(jnp.float32)
        return jnp.concatenate([moved[:, :1] + moved[:, 1:2], moved[:, 2:]], axis=1)

    total_rows = jnp.broadcast_to(cumulated[-1][:, None, :, None], (key_heads, 1, group_size, head_size))
    own_entry = jnp.concatenate([total_rows, fresh_state], axis=1)
    entry = chain(chain(sent_along(own_entry, 3), sent_along(own_entry, 2)), sent_along(own_entry, 1))
    reach = 3
    while reach < shards:
        entry = chain(sent_along(entry, reach), entry)
        reach *= 2
    incoming = entry[:, 1:]

    query_narrow = queries[0].reshape(row_count, key_heads, group_size, head_size)
    query_wide = query_narrow.astype(jnp.float32)
    products = jnp.einsum(
        "rgjd,sgd->gjrs", query_narrow, masked_keys, preferred_element_type=jnp.float32
    )
    ordered = cumulated.transpose(1, 2, 0)
    spread = ordered[..., :, None] - ordered[..., None, :]
    triangle = positions[:, None] >= positions[None, :]
    damping = jnp.where(triangle, jnp.exp(jnp.minimum(spread, 0.0)), 0.0)
    intra = jnp.einsum(
        "gjrs,sgje->rgje", products * damping, value_rows, precision=lax.Precision.HIGHEST
    )
    inter = (
        jnp.einsum("rgjd,gdje->rgje", query_wide, incoming, precision=lax.Precision.HIGHEST)
        * jnp.exp(cumulated)[..., None]
    )
    mixed = (inter + intra).reshape(row_count, query_head_rows, head_size)
    scaled = mixed * lax.rsqrt(jnp.mean(mixed * mixed, axis=-1, keepdims=True) + 1e-05)
    gating = spike_counts.astype(jnp.float32).reshape(
        row_count, query_head_rows, head_size
    ) * thresholds.reshape(query_head_rows, head_size)
    gated = jnp.where(
        valid_rows[:, None],
        (scaled * gating).reshape(row_count, query_head_rows * head_size),
        0.0,
    ).astype(jnp.bfloat16)
    head_outputs = jnp.where(section_index == 0, attention, gated)[None]
    return (head_outputs, local_activations)


def solution(mesh):
    return jax.shard_map(
        body,
        mesh=mesh,
        in_specs=(
            P("ctx", "tp"),
            P("section", "ctx", "tp"),
            P("section", "ctx", "tp"),
            P("ctx", "tp"),
            P("section", "tp", None),
            P(),
            P("ctx", "tp"),
            P("ctx", "tp"),
            P("tp"),
            P(),
        ),
        out_specs=(P("section", "ctx", "tp"), P("ctx", "tp")),
        check_vma=False,
    )
```

```python
import math

import jax
import jax.numpy as jnp
from jax import lax
from jax.sharding import PartitionSpec as P

HEAD = 128
WINDOW = 4096


def passed_along(x, by, section):
    shards = lax.axis_size("ctx")
    sections = lax.axis_size("section")
    pairs = [
        (i * sections + section, (i + by) * sections + section)
        for i in range(shards)
        if 0 <= i + by < shards
    ]
    return lax.ppermute(x, ("ctx", "section"), pairs)


def body(
    residual,
    queries,
    keys,
    window_values,
    mixing,
    norm_gain,
    log_decay,
    spike_counts,
    thresholds,
    lengths,
):
    section_index = lax.axis_index("section")
    shard_index = lax.axis_index("ctx")
    shards = lax.axis_size("ctx")
    row_count = keys.shape[1]
    head_size = HEAD
    key_heads = keys.shape[2] // head_size
    query_head_rows = queries.shape[2] // head_size
    group_size = query_head_rows // key_heads
    span_blocks = WINDOW // row_count
    feature_count = mixing.shape[2]
    scale = 1.0 / math.sqrt(head_size)
    positions = jnp.arange(row_count, dtype=jnp.int32)
    valid_rows = positions < lengths[shard_index]
    own_keys = keys[0]

    key_width = own_keys.shape[1]
    query_width = queries.shape[2]
    mate_copy = lax.ppermute(
        jnp.concatenate([queries[0], own_keys], axis=1), "section", [(0, 1)]
    )
    first_queries = jnp.where(section_index == 0, queries[0], mate_copy[:, :query_width])
    first_keys = jnp.where(section_index == 0, own_keys, mate_copy[:, query_width:])
    query_rows = first_queries.reshape(row_count, key_heads, group_size, head_size)
    base_distance = positions[:, None] - positions[None, :]
    packed = jnp.concatenate([first_keys, window_values], axis=1)
    sections = lax.axis_size("section")
    plan = [(0, 1)] + [(2 * j, 2 * j + 1) for j in range(1, span_blocks // 2)]
    plan += [(2 * j, None) for j in range(span_blocks // 2, span_blocks // 2 + 1)]
    running = jnp.zeros((key_heads, group_size, row_count, head_size), jnp.float32)
    totals = jnp.zeros((key_heads, group_size, row_count), jnp.float32)
    best = jnp.full((key_heads, group_size, row_count), -1e30, jnp.float32)
    for first_distance, second_distance in plan:
        pairs = []
        for taken, owner in ((first_distance, 0), (second_distance, 1)):
            if taken:
                pairs += [
                    (i * sections + owner, (i + taken) * sections + owner)
                    for i in range(shards)
                    if i + taken < shards
                ]
        joined = lax.ppermute(packed, ("ctx", "section"), pairs)
        if first_distance == 0:
            joined = jnp.where(section_index == 0, packed, joined)
        key_block, value_block = joined[:, :key_width], joined[:, key_width:]
        distance_blocks = jnp.where(
            section_index == 0,
            first_distance,
            span_blocks + 1 if second_distance is None else second_distance,
        )
        source = shard_index - distance_blocks
        key_valid = (source >= 0) & (positions < lengths[jnp.maximum(source, 0)])
        scores = (
            jnp.einsum(
                "rgjd,kgd->gjrk",
                query_rows,
                key_block.reshape(row_count, key_heads, head_size),
                preferred_element_type=jnp.float32,
            )
            * scale
        )
        distance = base_distance + distance_blocks * row_count
        allowed = key_valid[None, :] & (distance >= 0) & (distance < WINDOW)
        scores = jnp.where(allowed, scores, -1e30)
        new_best = jnp.maximum(best, jnp.max(scores, axis=-1))
        factor = jnp.exp(best - new_best)
        weights = jnp.where(allowed, jnp.exp(scores - new_best[..., None]), 0.0)
        blended = jnp.einsum(
            "gjrk,kgd->gjrd",
            weights.astype(jnp.bfloat16),
            value_block.reshape(row_count, key_heads, head_size),
            preferred_element_type=jnp.float32,
        )
        running = running * factor[..., None] + blended
        totals = totals * factor + jnp.sum(weights, axis=-1)
        best = new_best
    partial = lax.ppermute(
        jnp.concatenate([running, totals[..., None], best[..., None]], axis=-1),
        "section",
        [(1, 0)],
    )
    other_best = partial[..., head_size + 1]
    merged_best = jnp.maximum(best, other_best)
    own_factor = jnp.exp(best - merged_best)
    other_factor = jnp.exp(other_best - merged_best)
    running = running * own_factor[..., None] + partial[..., :head_size] * other_factor[..., None]
    totals = totals * own_factor + partial[..., head_size] * other_factor
    attention = running / jnp.maximum(totals, 1.0)[..., None]
    attention = attention.transpose(2, 0, 1, 3).reshape(row_count, query_head_rows * head_size)
    attention = jnp.where(valid_rows[:, None], attention, 0.0).astype(jnp.bfloat16)
    projected = jnp.dot(attention, mixing[0], preferred_element_type=jnp.float32)

    members = lax.axis_size("tp")
    member = lax.axis_index("tp")
    width = feature_count // members
    terms = projected.astype(jnp.bfloat16)
    summed = residual.astype(jnp.float32) + lax.dynamic_slice_in_dim(
        terms, member * width, width, 1
    ).astype(jnp.float32)
    for step in range(1, members):
        target = (member + step) % members
        sent = lax.dynamic_slice_in_dim(terms, target * width, width, 1)
        pairs = [(m, (m + step) % members) for m in range(members)]
        summed = summed + lax.ppermute(sent, ("section", "tp"), pairs).astype(jnp.float32)
    own_hidden = summed.astype(jnp.bfloat16)
    arrived = jnp.stack(
        [
            lax.ppermute(
                own_hidden,
                ("section", "tp"),
                [(m, members + (m + step) % members) for m in range(members)],
            )
            for step in range(members)
        ],
        0,
    )
    local_activations = jnp.where(section_index == 0, own_hidden, arrived[0])
    order = (member - jnp.arange(members, dtype=jnp.int32)) % members
    complete_hidden_matrix = (
        jnp.take(arrived, order, axis=0).transpose(1, 0, 2).reshape(row_count, feature_count)
    )

    masked_keys = jnp.where(valid_rows[:, None], own_keys, jnp.zeros_like(own_keys)).reshape(
        row_count, key_heads, head_size
    )
    wide_keys = masked_keys.astype(jnp.float32)
    decays = log_decay * valid_rows[:, None].astype(jnp.float32)
    wide = complete_hidden_matrix.astype(jnp.float32)
    normed = (
        wide
        * lax.rsqrt(jnp.mean(wide * wide, axis=-1, keepdims=True) + 1e-05)
        * norm_gain.astype(jnp.float32)
    ).astype(jnp.bfloat16)
    payload_vectors = lax.dot_general(
        normed, mixing[0], (((1,), (1,)), ((), ())), preferred_element_type=jnp.float32
    ).astype(jnp.bfloat16)
    cumulated = jnp.cumsum(decays, axis=0).reshape(row_count, key_heads, group_size)
    value_rows = payload_vectors.astype(jnp.float32).reshape(
        row_count, key_heads, group_size, head_size
    )
    fresh_state = jnp.einsum(
        "sgd,sgje->gdje",
        wide_keys,
        value_rows * jnp.exp(cumulated[-1] - cumulated)[..., None],
        precision=lax.Precision.HIGHEST,
    )

    def chain(previous_entry, latter):
        latter_total = latter[:, :1]
        return jnp.concatenate(
            [
                previous_entry[:, :1] + latter_total,
                previous_entry[:, 1:] * jnp.exp(latter_total) + latter[:, 1:],
            ],
            axis=1,
        )

    def sent_along(entry, by):
        total = entry[:, :1]
        high = total.astype(jnp.bfloat16)
        low = (total - high.astype(jnp.float32)).astype(jnp.bfloat16)
        narrow = jnp.concatenate([high, low, entry[:, 1:].astype(jnp.bfloat16)], axis=1)
        moved = passed_along(narrow, by, 1).astype(jnp.float32)
        return jnp.concatenate([moved[:, :1] + moved[:, 1:2], moved[:, 2:]], axis=1)

    total_rows = jnp.broadcast_to(cumulated[-1][:, None, :, None], (key_heads, 1, group_size, head_size))
    own_entry = jnp.concatenate([total_rows, fresh_state], axis=1)
    entry = chain(chain(sent_along(own_entry, 3), sent_along(own_entry, 2)), sent_along(own_entry, 1))
    reach = 3
    while reach < shards:
        entry = chain(sent_along(entry, reach), entry)
        reach *= 2
    incoming = entry[:, 1:]

    query_narrow = queries[0].reshape(row_count, key_heads, group_size, head_size)
    query_wide = query_narrow.astype(jnp.float32)
    products = jnp.einsum(
        "rgjd,sgd->gjrs", query_narrow, masked_keys, preferred_element_type=jnp.float32
    )
    ordered = cumulated.transpose(1, 2, 0)
    spread = ordered[..., :, None] - ordered[..., None, :]
    triangle = positions[:, None] >= positions[None, :]
    damping = jnp.where(triangle, jnp.exp(jnp.minimum(spread, 0.0)), 0.0)
    intra = jnp.einsum(
        "gjrs,sgje->rgje", products * damping, value_rows, precision=lax.Precision.HIGHEST
    )
    inter = (
        jnp.einsum("rgjd,gdje->rgje", query_wide, incoming, precision=lax.Precision.HIGHEST)
        * jnp.exp(cumulated)[..., None]
    )
    mixed = (inter + intra).reshape(row_count, query_head_rows, head_size)
    scaled = mixed * lax.rsqrt(jnp.mean(mixed * mixed, axis=-1, keepdims=True) + 1e-05)
    gating = spike_counts.astype(jnp.float32).reshape(
        row_count, query_head_rows, head_size
    ) * thresholds.reshape(query_head_rows, head_size)
    gated = jnp.where(
        valid_rows[:, None],
        (scaled * gating).reshape(row_count, query_head_rows * head_size),
        0.0,
    ).astype(jnp.bfloat16)
    head_outputs = jnp.where(section_index == 0, attention, gated)[None]
    return (head_outputs, local_activations)


def solution(mesh):
    return jax.shard_map(
        body,
        mesh=mesh,
        in_specs=(
            P("ctx", "tp"),
            P("section", "ctx", "tp"),
            P("section", "ctx", "tp"),
            P("ctx", "tp"),
            P("section", "tp", None),
            P(),
            P("ctx", "tp"),
            P("ctx", "tp"),
            P("tp"),
            P(),
        ),
        out_specs=(P("section", "ctx", "tp"), P("ctx", "tp")),
        check_vma=False,
    )
```

```python
import math

import jax
import jax.numpy as jnp
from jax import lax
from jax.sharding import PartitionSpec as P

HEAD = 128
WINDOW = 4096


def passed_along(x, by, section):
    shards = lax.axis_size("ctx")
    sections = lax.axis_size("section")
    pairs = [
        (i * sections + section, (i + by) * sections + section)
        for i in range(shards)
        if 0 <= i + by < shards
    ]
    return lax.ppermute(x, ("ctx", "section"), pairs)


def body(
    residual,
    queries,
    keys,
    window_values,
    mixing,
    norm_gain,
    log_decay,
    spike_counts,
    thresholds,
    lengths,
):
    section_index = lax.axis_index("section")
    shard_index = lax.axis_index("ctx")
    shards = lax.axis_size("ctx")
    row_count = keys.shape[1]
    head_size = HEAD
    key_heads = keys.shape[2] // head_size
    query_head_rows = queries.shape[2] // head_size
    group_size = query_head_rows // key_heads
    span_blocks = WINDOW // row_count
    feature_count = mixing.shape[2]
    scale = 1.0 / math.sqrt(head_size)
    positions = jnp.arange(row_count, dtype=jnp.int32)
    valid_rows = positions < lengths[shard_index]
    own_keys = keys[0]

    key_width = own_keys.shape[1]
    query_width = queries.shape[2]
    mate_copy = lax.ppermute(
        jnp.concatenate([queries[0], own_keys], axis=1), "section", [(0, 1)]
    )
    first_queries = jnp.where(section_index == 0, queries[0], mate_copy[:, :query_width])
    first_keys = jnp.where(section_index == 0, own_keys, mate_copy[:, query_width:])
    query_rows = first_queries.reshape(row_count, key_heads, group_size, head_size)
    base_distance = positions[:, None] - positions[None, :]
    packed = jnp.concatenate([first_keys, window_values], axis=1)
    sections = lax.axis_size("section")
    plan = [(0, 1)] + [(2 * j, 2 * j + 1) for j in range(1, span_blocks // 2)]
    plan += [(2 * j, None) for j in range(span_blocks // 2, span_blocks // 2 + 1)]
    running = jnp.zeros((key_heads, group_size, row_count, head_size), jnp.float32)
    totals = jnp.zeros((key_heads, group_size, row_count), jnp.float32)
    best = jnp.full((key_heads, group_size, row_count), -1e30, jnp.float32)
    for first_distance, second_distance in plan:
        pairs = []
        for taken, owner in ((first_distance, 0), (second_distance, 1)):
            if taken:
                pairs += [
                    (i * sections + owner, (i + taken) * sections + owner)
                    for i in range(shards)
                    if i + taken < shards
                ]
        joined = lax.ppermute(packed, ("ctx", "section"), pairs)
        if first_distance == 0:
            joined = jnp.where(section_index == 0, packed, joined)
        key_block, value_block = joined[:, :key_width], joined[:, key_width:]
        distance_blocks = jnp.where(
            section_index == 0,
            first_distance,
            span_blocks + 1 if second_distance is None else second_distance,
        )
        source = shard_index - distance_blocks
        key_valid = (source >= 0) & (positions < lengths[jnp.maximum(source, 0)])
        scores = (
            jnp.einsum(
                "rgjd,kgd->gjrk",
                query_rows,
                key_block.reshape(row_count, key_heads, head_size),
                preferred_element_type=jnp.float32,
            )
            * scale
        )
        distance = base_distance + distance_blocks * row_count
        allowed = key_valid[None, :] & (distance >= 0) & (distance < WINDOW)
        scores = jnp.where(allowed, scores, -1e30)
        new_best = jnp.maximum(best, jnp.max(scores, axis=-1))
        factor = jnp.exp(best - new_best)
        weights = jnp.where(allowed, jnp.exp(scores - new_best[..., None]), 0.0)
        blended = jnp.einsum(
            "gjrk,kgd->gjrd",
            weights.astype(jnp.bfloat16),
            value_block.reshape(row_count, key_heads, head_size),
            preferred_element_type=jnp.float32,
        )
        running = running * factor[..., None] + blended
        totals = totals * factor + jnp.sum(weights, axis=-1)
        best = new_best
    partial = lax.ppermute(
        jnp.concatenate([running, totals[..., None], best[..., None]], axis=-1),
        "section",
        [(1, 0)],
    )
    other_best = partial[..., head_size + 1]
    merged_best = jnp.maximum(best, other_best)
    own_factor = jnp.exp(best - merged_best)
    other_factor = jnp.exp(other_best - merged_best)
    running = running * own_factor[..., None] + partial[..., :head_size] * other_factor[..., None]
    totals = totals * own_factor + partial[..., head_size] * other_factor
    attention = running / jnp.maximum(totals, 1.0)[..., None]
    attention = attention.transpose(2, 0, 1, 3).reshape(row_count, query_head_rows * head_size)
    attention = jnp.where(valid_rows[:, None], attention, 0.0).astype(jnp.bfloat16)
    projected = jnp.dot(attention, mixing[0], preferred_element_type=jnp.float32)

    members = lax.axis_size("tp")
    member = lax.axis_index("tp")
    width = feature_count // members
    terms = projected.astype(jnp.bfloat16)
    summed = residual.astype(jnp.float32) + lax.dynamic_slice_in_dim(
        terms, member * width, width, 1
    ).astype(jnp.float32)
    for step in range(1, members):
        target = (member + step) % members
        sent = lax.dynamic_slice_in_dim(terms, target * width, width, 1)
        pairs = [(m, (m + step) % members) for m in range(members)]
        summed = summed + lax.ppermute(sent, ("section", "tp"), pairs).astype(jnp.float32)
    own_hidden = summed.astype(jnp.bfloat16)
    arrived = jnp.stack(
        [
            lax.ppermute(
                own_hidden,
                ("section", "tp"),
                [(m, members + (m + step) % members) for m in range(members)],
            )
            for step in range(members)
        ],
        0,
    )
    local_activations = jnp.where(section_index == 0, own_hidden, arrived[0])
    order = (member - jnp.arange(members, dtype=jnp.int32)) % members
    complete_hidden_matrix = (
        jnp.take(arrived, order, axis=0).transpose(1, 0, 2).reshape(row_count, feature_count)
    )

    masked_keys = jnp.where(valid_rows[:, None], own_keys, jnp.zeros_like(own_keys)).reshape(
        row_count, key_heads, head_size
    )
    wide_keys = masked_keys.astype(jnp.float32)
    decays = log_decay * valid_rows[:, None].astype(jnp.float32)
    wide = complete_hidden_matrix.astype(jnp.float32)
    normed = (
        wide
        * lax.rsqrt(jnp.mean(wide * wide, axis=-1, keepdims=True) + 1e-05)
        * norm_gain.astype(jnp.float32)
    ).astype(jnp.bfloat16)
    payload_vectors = lax.dot_general(
        normed, mixing[0], (((1,), (1,)), ((), ())), preferred_element_type=jnp.float32
    ).astype(jnp.bfloat16)
    cumulated = jnp.cumsum(decays, axis=0).reshape(row_count, key_heads, group_size)
    value_rows = payload_vectors.astype(jnp.float32).reshape(
        row_count, key_heads, group_size, head_size
    )
    fresh_state = jnp.einsum(
        "sgd,sgje->gdje",
        wide_keys,
        value_rows * jnp.exp(cumulated[-1] - cumulated)[..., None],
        precision=lax.Precision.HIGHEST,
    )

    def chain(previous_entry, latter):
        latter_total = latter[:, :1]
        return jnp.concatenate(
            [
                previous_entry[:, :1] + latter_total,
                previous_entry[:, 1:] * jnp.exp(latter_total) + latter[:, 1:],
            ],
            axis=1,
        )

    def sent_along(entry, by):
        total = entry[:, :1]
        high = total.astype(jnp.bfloat16)
        low = (total - high.astype(jnp.float32)).astype(jnp.bfloat16)
        narrow = jnp.concatenate([high, low, entry[:, 1:].astype(jnp.bfloat16)], axis=1)
        moved = passed_along(narrow, by, 1).astype(jnp.float32)
        return jnp.concatenate([moved[:, :1] + moved[:, 1:2], moved[:, 2:]], axis=1)

    total_rows = jnp.broadcast_to(cumulated[-1][:, None, :, None], (key_heads, 1, group_size, head_size))
    own_entry = jnp.concatenate([total_rows, fresh_state], axis=1)
    entry = sent_along(own_entry, 1)
    for times in range(2, 5):
        entry = chain(sent_along(own_entry, times), entry)
    reach = 4
    while reach < shards:
        spread = 4 if reach < 16 else -(-shards // reach)
        joined = entry
        for times in range(1, spread):
            joined = chain(sent_along(entry, times * reach), joined)
        entry = joined
        reach *= spread
    incoming = entry[:, 1:]

    query_narrow = queries[0].reshape(row_count, key_heads, group_size, head_size)
    query_wide = query_narrow.astype(jnp.float32)
    products = jnp.einsum(
        "rgjd,sgd->gjrs", query_narrow, masked_keys, preferred_element_type=jnp.float32
    )
    ordered = cumulated.transpose(1, 2, 0)
    spread = ordered[..., :, None] - ordered[..., None, :]
    triangle = positions[:, None] >= positions[None, :]
    damping = jnp.where(triangle, jnp.exp(jnp.minimum(spread, 0.0)), 0.0)
    intra = jnp.einsum(
        "gjrs,sgje->rgje", products * damping, value_rows, precision=lax.Precision.HIGHEST
    )
    inter = (
        jnp.einsum("rgjd,gdje->rgje", query_wide, incoming, precision=lax.Precision.HIGHEST)
        * jnp.exp(cumulated)[..., None]
    )
    mixed = (inter + intra).reshape(row_count, query_head_rows, head_size)
    scaled = mixed * lax.rsqrt(jnp.mean(mixed * mixed, axis=-1, keepdims=True) + 1e-05)
    gating = spike_counts.astype(jnp.float32).reshape(
        row_count, query_head_rows, head_size
    ) * thresholds.reshape(query_head_rows, head_size)
    gated = jnp.where(
        valid_rows[:, None],
        (scaled * gating).reshape(row_count, query_head_rows * head_size),
        0.0,
    ).astype(jnp.bfloat16)
    head_outputs = jnp.where(section_index == 0, attention, gated)[None]
    return (head_outputs, local_activations)


def solution(mesh):
    return jax.shard_map(
        body,
        mesh=mesh,
        in_specs=(
            P("ctx", "tp"),
            P("section", "ctx", "tp"),
            P("section", "ctx", "tp"),
            P("ctx", "tp"),
            P("section", "tp", None),
            P(),
            P("ctx", "tp"),
            P("ctx", "tp"),
            P("tp"),
            P(),
        ),
        out_specs=(P("section", "ctx", "tp"), P("ctx", "tp")),
        check_vma=False,
    )
```

```python
import math

import jax
import jax.numpy as jnp
from jax import lax
from jax.sharding import PartitionSpec as P

HEAD = 128
WINDOW = 4096


def passed_along(x, by, section):
    shards = lax.axis_size("ctx")
    sections = lax.axis_size("section")
    pairs = [
        (i * sections + section, (i + by) * sections + section)
        for i in range(shards)
        if 0 <= i + by < shards
    ]
    return lax.ppermute(x, ("ctx", "section"), pairs)


def body(
    residual,
    queries,
    keys,
    window_values,
    mixing,
    norm_gain,
    log_decay,
    spike_counts,
    thresholds,
    lengths,
):
    section_index = lax.axis_index("section")
    shard_index = lax.axis_index("ctx")
    shards = lax.axis_size("ctx")
    row_count = keys.shape[1]
    head_size = HEAD
    key_heads = keys.shape[2] // head_size
    query_head_rows = queries.shape[2] // head_size
    group_size = query_head_rows // key_heads
    span_blocks = WINDOW // row_count
    feature_count = mixing.shape[2]
    scale = 1.0 / math.sqrt(head_size)
    positions = jnp.arange(row_count, dtype=jnp.int32)
    valid_rows = positions < lengths[shard_index]
    own_keys = keys[0]

    key_width = own_keys.shape[1]
    query_width = queries.shape[2]
    mate_copy = lax.ppermute(
        jnp.concatenate([queries[0], own_keys], axis=1), "section", [(0, 1)]
    )
    first_queries = jnp.where(section_index == 0, queries[0], mate_copy[:, :query_width])
    first_keys = jnp.where(section_index == 0, own_keys, mate_copy[:, query_width:])
    query_rows = first_queries.reshape(row_count, key_heads, group_size, head_size)
    base_distance = positions[:, None] - positions[None, :]
    packed = jnp.concatenate([first_keys, window_values], axis=1)
    sections = lax.axis_size("section")
    plan = [(0, 1)] + [(2 * j, 2 * j + 1) for j in range(1, span_blocks // 2)]
    plan += [(2 * j, None) for j in range(span_blocks // 2, span_blocks // 2 + 1)]
    running = jnp.zeros((key_heads, group_size, row_count, head_size), jnp.float32)
    totals = jnp.zeros((key_heads, group_size, row_count), jnp.float32)
    best = jnp.full((key_heads, group_size, row_count), -1e30, jnp.float32)
    for first_distance, second_distance in plan:
        pairs = []
        for taken, owner in ((first_distance, 0), (second_distance, 1)):
            if taken:
                pairs += [
                    (i * sections + owner, (i + taken) * sections + owner)
                    for i in range(shards)
                    if i + taken < shards
                ]
        joined = lax.ppermute(packed, ("ctx", "section"), pairs)
        if first_distance == 0:
            joined = jnp.where(section_index == 0, packed, joined)
        key_block, value_block = joined[:, :key_width], joined[:, key_width:]
        distance_blocks = jnp.where(
            section_index == 0,
            first_distance,
            span_blocks + 1 if second_distance is None else second_distance,
        )
        source = shard_index - distance_blocks
        key_valid = (source >= 0) & (positions < lengths[jnp.maximum(source, 0)])
        scores = (
            jnp.einsum(
                "rgjd,kgd->gjrk",
                query_rows,
                key_block.reshape(row_count, key_heads, head_size),
                preferred_element_type=jnp.float32,
            )
            * scale
        )
        distance = base_distance + distance_blocks * row_count
        allowed = key_valid[None, :] & (distance >= 0) & (distance < WINDOW)
        scores = jnp.where(allowed, scores, -1e30)
        new_best = jnp.maximum(best, jnp.max(scores, axis=-1))
        factor = jnp.exp(best - new_best)
        weights = jnp.where(allowed, jnp.exp(scores - new_best[..., None]), 0.0)
        blended = jnp.einsum(
            "gjrk,kgd->gjrd",
            weights.astype(jnp.bfloat16),
            value_block.reshape(row_count, key_heads, head_size),
            preferred_element_type=jnp.float32,
        )
        running = running * factor[..., None] + blended
        totals = totals * factor + jnp.sum(weights, axis=-1)
        best = new_best
    partial = lax.ppermute(
        jnp.concatenate([running, totals[..., None], best[..., None]], axis=-1),
        "section",
        [(1, 0)],
    )
    other_best = partial[..., head_size + 1]
    merged_best = jnp.maximum(best, other_best)
    own_factor = jnp.exp(best - merged_best)
    other_factor = jnp.exp(other_best - merged_best)
    running = running * own_factor[..., None] + partial[..., :head_size] * other_factor[..., None]
    totals = totals * own_factor + partial[..., head_size] * other_factor
    attention = running / jnp.maximum(totals, 1.0)[..., None]
    attention = attention.transpose(2, 0, 1, 3).reshape(row_count, query_head_rows * head_size)
    attention = jnp.where(valid_rows[:, None], attention, 0.0).astype(jnp.bfloat16)
    projected = jnp.dot(attention, mixing[0], preferred_element_type=jnp.float32)

    members = lax.axis_size("tp")
    member = lax.axis_index("tp")
    width = feature_count // members
    terms = projected.astype(jnp.bfloat16)
    summed = residual.astype(jnp.float32) + lax.dynamic_slice_in_dim(
        terms, member * width, width, 1
    ).astype(jnp.float32)
    for step in range(1, members):
        target = (member + step) % members
        sent = lax.dynamic_slice_in_dim(terms, target * width, width, 1)
        pairs = [(m, (m + step) % members) for m in range(members)]
        summed = summed + lax.ppermute(sent, ("section", "tp"), pairs).astype(jnp.float32)
    own_hidden = summed.astype(jnp.bfloat16)
    arrived = jnp.stack(
        [
            lax.ppermute(
                own_hidden,
                ("section", "tp"),
                [(m, members + (m + step) % members) for m in range(members)],
            )
            for step in range(members)
        ],
        0,
    )
    local_activations = jnp.where(section_index == 0, own_hidden, arrived[0])

    masked_keys = jnp.where(valid_rows[:, None], own_keys, jnp.zeros_like(own_keys)).reshape(
        row_count, key_heads, head_size
    )
    wide_keys = masked_keys.astype(jnp.float32)
    decays = log_decay * valid_rows[:, None].astype(jnp.float32)
    wide = arrived.astype(jnp.float32)
    inverse_scale = lax.rsqrt(
        jnp.sum(wide * wide, axis=(0, 2))[:, None] / feature_count + 1e-05
    )
    payload_sum = jnp.zeros((row_count, mixing.shape[1]), jnp.float32)
    for step in range(members):
        owner = (member - step) % members
        gain = lax.dynamic_slice_in_dim(norm_gain, owner * width, width, 0).astype(jnp.float32)
        normed = (wide[step] * inverse_scale * gain).astype(jnp.bfloat16)
        payload_sum = payload_sum + lax.dot_general(
            normed,
            lax.dynamic_slice_in_dim(mixing[0], owner * width, width, 1),
            (((1,), (1,)), ((), ())),
            preferred_element_type=jnp.float32,
        )
    payload_vectors = payload_sum.astype(jnp.bfloat16)
    cumulated = jnp.cumsum(decays, axis=0).reshape(row_count, key_heads, group_size)
    value_rows = payload_vectors.astype(jnp.float32).reshape(
        row_count, key_heads, group_size, head_size
    )
    fresh_state = jnp.einsum(
        "sgd,sgje->gdje",
        wide_keys,
        value_rows * jnp.exp(cumulated[-1] - cumulated)[..., None],
        precision=lax.Precision.HIGHEST,
    )

    def chain(previous_entry, latter):
        latter_total = latter[:, :1]
        return jnp.concatenate(
            [
                previous_entry[:, :1] + latter_total,
                previous_entry[:, 1:] * jnp.exp(latter_total) + latter[:, 1:],
            ],
            axis=1,
        )

    def sent_along(entry, by):
        total = entry[:, :1]
        high = total.astype(jnp.bfloat16)
        low = (total - high.astype(jnp.float32)).astype(jnp.bfloat16)
        narrow = jnp.concatenate([high, low, entry[:, 1:].astype(jnp.bfloat16)], axis=1)
        moved = passed_along(narrow, by, 1).astype(jnp.float32)
        return jnp.concatenate([moved[:, :1] + moved[:, 1:2], moved[:, 2:]], axis=1)

    total_rows = jnp.broadcast_to(cumulated[-1][:, None, :, None], (key_heads, 1, group_size, head_size))
    own_entry = jnp.concatenate([total_rows, fresh_state], axis=1)
    entry = sent_along(own_entry, 1)
    for times in range(2, 4):
        entry = chain(sent_along(own_entry, times), entry)
    reach = 3
    while reach < shards:
        spread = 4 if reach < 12 else -(-shards // reach)
        joined = entry
        for times in range(1, spread):
            joined = chain(sent_along(entry, times * reach), joined)
        entry = joined
        reach *= spread
    incoming = entry[:, 1:]

    query_narrow = queries[0].reshape(row_count, key_heads, group_size, head_size)
    query_wide = query_narrow.astype(jnp.float32)
    products = jnp.einsum(
        "rgjd,sgd->gjrs", query_narrow, masked_keys, preferred_element_type=jnp.float32
    )
    ordered = cumulated.transpose(1, 2, 0)
    spread = ordered[..., :, None] - ordered[..., None, :]
    triangle = positions[:, None] >= positions[None, :]
    damping = jnp.where(triangle, jnp.exp(jnp.minimum(spread, 0.0)), 0.0)
    intra = jnp.einsum(
        "gjrs,sgje->rgje", products * damping, value_rows, precision=lax.Precision.HIGHEST
    )
    inter = (
        jnp.einsum("rgjd,gdje->rgje", query_wide, incoming, precision=lax.Precision.HIGHEST)
        * jnp.exp(cumulated)[..., None]
    )
    mixed = (inter + intra).reshape(row_count, query_head_rows, head_size)
    scaled = mixed * lax.rsqrt(jnp.mean(mixed * mixed, axis=-1, keepdims=True) + 1e-05)
    gating = spike_counts.astype(jnp.float32).reshape(
        row_count, query_head_rows, head_size
    ) * thresholds.reshape(query_head_rows, head_size)
    gated = jnp.where(
        valid_rows[:, None],
        (scaled * gating).reshape(row_count, query_head_rows * head_size),
        0.0,
    ).astype(jnp.bfloat16)
    head_outputs = jnp.where(section_index == 0, attention, gated)[None]
    return (head_outputs, local_activations)


def solution(mesh):
    return jax.shard_map(
        body,
        mesh=mesh,
        in_specs=(
            P("ctx", "tp"),
            P("section", "ctx", "tp"),
            P("section", "ctx", "tp"),
            P("ctx", "tp"),
            P("section", "tp", None),
            P(),
            P("ctx", "tp"),
            P("ctx", "tp"),
            P("tp"),
            P(),
        ),
        out_specs=(P("section", "ctx", "tp"), P("ctx", "tp")),
        check_vma=False,
    )
```

```python
import math

import jax
import jax.numpy as jnp
from jax import lax
from jax.sharding import PartitionSpec as P

HEAD = 128
WINDOW = 4096


def passed_along(x, by, section):
    shards = lax.axis_size("ctx")
    sections = lax.axis_size("section")
    pairs = [
        (i * sections + section, (i + by) * sections + section)
        for i in range(shards)
        if 0 <= i + by < shards
    ]
    return lax.ppermute(x, ("ctx", "section"), pairs)


def body(
    residual,
    queries,
    keys,
    window_values,
    mixing,
    norm_gain,
    log_decay,
    spike_counts,
    thresholds,
    lengths,
):
    section_index = lax.axis_index("section")
    shard_index = lax.axis_index("ctx")
    shards = lax.axis_size("ctx")
    row_count = keys.shape[1]
    head_size = HEAD
    key_heads = keys.shape[2] // head_size
    query_head_rows = queries.shape[2] // head_size
    group_size = query_head_rows // key_heads
    span_blocks = WINDOW // row_count
    feature_count = mixing.shape[2]
    scale = 1.0 / math.sqrt(head_size)
    positions = jnp.arange(row_count, dtype=jnp.int32)
    valid_rows = positions < lengths[shard_index]
    own_keys = keys[0]

    key_width = own_keys.shape[1]
    query_width = queries.shape[2]
    mate_copy = lax.ppermute(
        jnp.concatenate([queries[0], own_keys], axis=1), "section", [(0, 1)]
    )
    first_queries = jnp.where(section_index == 0, queries[0], mate_copy[:, :query_width])
    first_keys = jnp.where(section_index == 0, own_keys, mate_copy[:, query_width:])
    query_rows = first_queries.reshape(row_count, key_heads, group_size, head_size)
    base_distance = positions[:, None] - positions[None, :]
    packed = jnp.concatenate([first_keys, window_values], axis=1)
    sections = lax.axis_size("section")
    relay = 12
    bundled = (span_blocks - relay) // 2 + 1
    plan = [(2 * j, 2 * j + 1) for j in range(relay // 2)]
    running = jnp.zeros((key_heads, group_size, row_count, head_size), jnp.float32)
    totals = jnp.zeros((key_heads, group_size, row_count), jnp.float32)
    best = jnp.full((key_heads, group_size, row_count), -1e30, jnp.float32)

    def blend(carry, joined, distance_blocks):
        running, totals, best = carry
        key_block, value_block = joined[:, :key_width], joined[:, key_width:]
        source = shard_index - distance_blocks
        key_valid = (source >= 0) & (positions < lengths[jnp.clip(source, 0, shards - 1)])
        scores = (
            jnp.einsum(
                "rgjd,kgd->gjrk",
                query_rows,
                key_block.reshape(row_count, key_heads, head_size),
                preferred_element_type=jnp.float32,
            )
            * scale
        )
        distance = base_distance + distance_blocks * row_count
        allowed = key_valid[None, :] & (distance >= 0) & (distance < WINDOW)
        scores = jnp.where(allowed, scores, -1e30)
        new_best = jnp.maximum(best, jnp.max(scores, axis=-1))
        factor = jnp.exp(best - new_best)
        weights = jnp.where(allowed, jnp.exp(scores - new_best[..., None]), 0.0)
        blended = jnp.einsum(
            "gjrk,kgd->gjrd",
            weights.astype(jnp.bfloat16),
            value_block.reshape(row_count, key_heads, head_size),
            preferred_element_type=jnp.float32,
        )
        return (
            running * factor[..., None] + blended,
            totals * factor + jnp.sum(weights, axis=-1),
            new_best,
        )

    def both_pairs(first_distance, second_distance):
        pairs = []
        for taken, owner in ((first_distance, 0), (second_distance, 1)):
            if taken:
                pairs += [
                    (i * sections + owner, (i + taken) * sections + owner)
                    for i in range(shards)
                    if i + taken < shards
                ]
        return pairs

    carry = (running, totals, best)
    held = []
    for first_distance, second_distance in plan:
        joined = lax.ppermute(packed, ("ctx", "section"), both_pairs(first_distance, second_distance))
        if first_distance == 0:
            joined = jnp.where(section_index == 0, packed, joined)
        held.append(joined)
        carry = blend(carry, joined, jnp.where(section_index == 0, first_distance, second_distance))
    bundle = lax.ppermute(
        jnp.concatenate(held[:bundled], axis=1), ("ctx", "section"), both_pairs(relay, relay)
    )
    for slot in range(bundled):
        carry = blend(
            carry,
            bundle[:, slot * 2 * key_width:(slot + 1) * 2 * key_width],
            relay + 2 * slot + jnp.where(section_index == 0, 0, 1),
        )
    running, totals, best = carry
    partial = lax.ppermute(
        jnp.concatenate([running, totals[..., None], best[..., None]], axis=-1),
        "section",
        [(1, 0)],
    )
    other_best = partial[..., head_size + 1]
    merged_best = jnp.maximum(best, other_best)
    own_factor = jnp.exp(best - merged_best)
    other_factor = jnp.exp(other_best - merged_best)
    running = running * own_factor[..., None] + partial[..., :head_size] * other_factor[..., None]
    totals = totals * own_factor + partial[..., head_size] * other_factor
    attention = running / jnp.maximum(totals, 1.0)[..., None]
    attention = attention.transpose(2, 0, 1, 3).reshape(row_count, query_head_rows * head_size)
    attention = jnp.where(valid_rows[:, None], attention, 0.0).astype(jnp.bfloat16)
    projected = jnp.dot(attention, mixing[0], preferred_element_type=jnp.float32)

    members = lax.axis_size("tp")
    member = lax.axis_index("tp")
    width = feature_count // members
    terms = projected.astype(jnp.bfloat16)
    summed = residual.astype(jnp.float32) + lax.dynamic_slice_in_dim(
        terms, member * width, width, 1
    ).astype(jnp.float32)
    for step in range(1, members):
        target = (member + step) % members
        sent = lax.dynamic_slice_in_dim(terms, target * width, width, 1)
        pairs = [(m, (m + step) % members) for m in range(members)]
        summed = summed + lax.ppermute(sent, ("section", "tp"), pairs).astype(jnp.float32)
    own_hidden = summed.astype(jnp.bfloat16)
    arrived = jnp.stack(
        [
            lax.ppermute(
                own_hidden,
                ("section", "tp"),
                [(m, members + (m + step) % members) for m in range(members)],
            )
            for step in range(members)
        ],
        0,
    )
    local_activations = jnp.where(section_index == 0, own_hidden, arrived[0])

    masked_keys = jnp.where(valid_rows[:, None], own_keys, jnp.zeros_like(own_keys)).reshape(
        row_count, key_heads, head_size
    )
    wide_keys = masked_keys.astype(jnp.float32)
    decays = log_decay * valid_rows[:, None].astype(jnp.float32)
    wide = arrived.astype(jnp.float32)
    inverse_scale = lax.rsqrt(
        jnp.sum(wide * wide, axis=(0, 2))[:, None] / feature_count + 1e-05
    )
    payload_sum = jnp.zeros((row_count, mixing.shape[1]), jnp.float32)
    for step in range(members):
        owner = (member - step) % members
        gain = lax.dynamic_slice_in_dim(norm_gain, owner * width, width, 0).astype(jnp.float32)
        normed = (wide[step] * inverse_scale * gain).astype(jnp.bfloat16)
        payload_sum = payload_sum + lax.dot_general(
            normed,
            lax.dynamic_slice_in_dim(mixing[0], owner * width, width, 1),
            (((1,), (1,)), ((), ())),
            preferred_element_type=jnp.float32,
        )
    payload_vectors = payload_sum.astype(jnp.bfloat16)
    cumulated = jnp.cumsum(decays, axis=0).reshape(row_count, key_heads, group_size)
    value_rows = payload_vectors.astype(jnp.float32).reshape(
        row_count, key_heads, group_size, head_size
    )
    fresh_state = jnp.einsum(
        "sgd,sgje->gdje",
        wide_keys,
        value_rows * jnp.exp(cumulated[-1] - cumulated)[..., None],
        precision=lax.Precision.HIGHEST,
    )

    def chain(previous_entry, latter):
        latter_total = latter[:, :1]
        return jnp.concatenate(
            [
                previous_entry[:, :1] + latter_total,
                previous_entry[:, 1:] * jnp.exp(latter_total) + latter[:, 1:],
            ],
            axis=1,
        )

    def sent_along(entry, by):
        total = entry[:, :1]
        high = total.astype(jnp.bfloat16)
        low = (total - high.astype(jnp.float32)).astype(jnp.bfloat16)
        narrow = jnp.concatenate([high, low, entry[:, 1:].astype(jnp.bfloat16)], axis=1)
        moved = passed_along(narrow, by, 1).astype(jnp.float32)
        return jnp.concatenate([moved[:, :1] + moved[:, 1:2], moved[:, 2:]], axis=1)

    total_rows = jnp.broadcast_to(cumulated[-1][:, None, :, None], (key_heads, 1, group_size, head_size))
    own_entry = jnp.concatenate([total_rows, fresh_state], axis=1)
    entry = sent_along(own_entry, 1)
    for times in range(2, 4):
        entry = chain(sent_along(own_entry, times), entry)
    reach = 3
    while reach < shards:
        spread = 4 if reach < 12 else -(-shards // reach)
        joined = entry
        for times in range(1, spread):
            joined = chain(sent_along(entry, times * reach), joined)
        entry = joined
        reach *= spread
    incoming = entry[:, 1:]

    query_narrow = queries[0].reshape(row_count, key_heads, group_size, head_size)
    query_wide = query_narrow.astype(jnp.float32)
    products = jnp.einsum(
        "rgjd,sgd->gjrs", query_narrow, masked_keys, preferred_element_type=jnp.float32
    )
    ordered = cumulated.transpose(1, 2, 0)
    spread = ordered[..., :, None] - ordered[..., None, :]
    triangle = positions[:, None] >= positions[None, :]
    damping = jnp.where(triangle, jnp.exp(jnp.minimum(spread, 0.0)), 0.0)
    intra = jnp.einsum(
        "gjrs,sgje->rgje", products * damping, value_rows, precision=lax.Precision.HIGHEST
    )
    inter = (
        jnp.einsum("rgjd,gdje->rgje", query_wide, incoming, precision=lax.Precision.HIGHEST)
        * jnp.exp(cumulated)[..., None]
    )
    mixed = (inter + intra).reshape(row_count, query_head_rows, head_size)
    scaled = mixed * lax.rsqrt(jnp.mean(mixed * mixed, axis=-1, keepdims=True) + 1e-05)
    gating = spike_counts.astype(jnp.float32).reshape(
        row_count, query_head_rows, head_size
    ) * thresholds.reshape(query_head_rows, head_size)
    gated = jnp.where(
        valid_rows[:, None],
        (scaled * gating).reshape(row_count, query_head_rows * head_size),
        0.0,
    ).astype(jnp.bfloat16)
    head_outputs = jnp.where(section_index == 0, attention, gated)[None]
    return (head_outputs, local_activations)


def solution(mesh):
    return jax.shard_map(
        body,
        mesh=mesh,
        in_specs=(
            P("ctx", "tp"),
            P("section", "ctx", "tp"),
            P("section", "ctx", "tp"),
            P("ctx", "tp"),
            P("section", "tp", None),
            P(),
            P("ctx", "tp"),
            P("ctx", "tp"),
            P("tp"),
            P(),
        ),
        out_specs=(P("section", "ctx", "tp"), P("ctx", "tp")),
        check_vma=False,
    )
```

```python
import math

import jax
import jax.numpy as jnp
from jax import lax
from jax.sharding import PartitionSpec as P

HEAD = 128
WINDOW = 4096


def passed_along(x, by, section):
    shards = lax.axis_size("ctx")
    sections = lax.axis_size("section")
    pairs = [
        (i * sections + section, (i + by) * sections + section)
        for i in range(shards)
        if 0 <= i + by < shards
    ]
    return lax.ppermute(x, ("ctx", "section"), pairs)


def body(
    residual,
    queries,
    keys,
    window_values,
    mixing,
    norm_gain,
    log_decay,
    spike_counts,
    thresholds,
    lengths,
):
    section_index = lax.axis_index("section")
    shard_index = lax.axis_index("ctx")
    shards = lax.axis_size("ctx")
    row_count = keys.shape[1]
    head_size = HEAD
    key_heads = keys.shape[2] // head_size
    query_head_rows = queries.shape[2] // head_size
    group_size = query_head_rows // key_heads
    span_blocks = WINDOW // row_count
    feature_count = mixing.shape[2]
    scale = 1.0 / math.sqrt(head_size)
    positions = jnp.arange(row_count, dtype=jnp.int32)
    valid_rows = positions < lengths[shard_index]
    own_keys = keys[0]

    key_width = own_keys.shape[1]
    query_width = queries.shape[2]
    mate_copy = lax.ppermute(
        jnp.concatenate([queries[0], own_keys], axis=1), "section", [(0, 1)]
    )
    first_queries = jnp.where(section_index == 0, queries[0], mate_copy[:, :query_width])
    first_keys = jnp.where(section_index == 0, own_keys, mate_copy[:, query_width:])
    query_rows = first_queries.reshape(row_count, key_heads, group_size, head_size)
    base_distance = positions[:, None] - positions[None, :]
    packed = jnp.concatenate([first_keys, window_values], axis=1)
    sections = lax.axis_size("section")
    relay = 12
    bundled = (span_blocks - relay) // 2 + 1
    plan = [(0, 1), (2, 3), (4, 9), (6, 11), (8, None), (10, None)]
    running = jnp.zeros((key_heads, group_size, row_count, head_size), jnp.float32)
    totals = jnp.zeros((key_heads, group_size, row_count), jnp.float32)
    best = jnp.full((key_heads, group_size, row_count), -1e30, jnp.float32)

    def blend(carry, joined, distance_blocks):
        running, totals, best = carry
        key_block, value_block = joined[:, :key_width], joined[:, key_width:]
        source = shard_index - distance_blocks
        key_valid = (source >= 0) & (positions < lengths[jnp.clip(source, 0, shards - 1)])
        scores = (
            jnp.einsum(
                "rgjd,kgd->gjrk",
                query_rows,
                key_block.reshape(row_count, key_heads, head_size),
                preferred_element_type=jnp.float32,
            )
            * scale
        )
        distance = base_distance + distance_blocks * row_count
        allowed = key_valid[None, :] & (distance >= 0) & (distance < WINDOW)
        scores = jnp.where(allowed, scores, -1e30)
        new_best = jnp.maximum(best, jnp.max(scores, axis=-1))
        factor = jnp.exp(best - new_best)
        weights = jnp.where(allowed, jnp.exp(scores - new_best[..., None]), 0.0)
        blended = jnp.einsum(
            "gjrk,kgd->gjrd",
            weights.astype(jnp.bfloat16),
            value_block.reshape(row_count, key_heads, head_size),
            preferred_element_type=jnp.float32,
        )
        return (
            running * factor[..., None] + blended,
            totals * factor + jnp.sum(weights, axis=-1),
            new_best,
        )

    def both_pairs(first_distance, second_distance):
        pairs = []
        for taken, owner in ((first_distance, 0), (second_distance, 1)):
            if taken:
                pairs += [
                    (i * sections + owner, (i + taken) * sections + owner)
                    for i in range(shards)
                    if i + taken < shards
                ]
        return pairs

    carry = (running, totals, best)
    held = []
    for first_distance, second_distance in plan:
        joined = lax.ppermute(packed, ("ctx", "section"), both_pairs(first_distance, second_distance))
        if first_distance == 0:
            joined = jnp.where(section_index == 0, packed, joined)
        held.append(joined)
        if second_distance is None:
            second_distance = span_blocks + 1
        carry = blend(carry, joined, jnp.where(section_index == 0, first_distance, second_distance))
    bundle = lax.ppermute(
        jnp.concatenate(held[:bundled], axis=1), ("ctx", "section"), both_pairs(relay, relay)
    )
    forwarded = lax.ppermute(
        jnp.concatenate(held[2:4], axis=1),
        ("ctx", "section"),
        [(i * sections, (i + 1) * sections + 1) for i in range(shards - 1)],
    )
    slots = [
        (bundle, 0, forwarded, 0, relay, 5),
        (bundle, 1, forwarded, 1, relay + 2, 7),
        (bundle, 2, bundle, 0, relay + 4, relay + 1),
        (bundle, 2, bundle, 1, span_blocks + 1, relay + 3),
    ]
    width_of = 2 * key_width
    for first_array, first_slot, second_array, second_slot, first_distance, second_distance in slots:
        joined = jnp.where(
            section_index == 0,
            first_array[:, first_slot * width_of:(first_slot + 1) * width_of],
            second_array[:, second_slot * width_of:(second_slot + 1) * width_of],
        )
        carry = blend(carry, joined, jnp.where(section_index == 0, first_distance, second_distance))
    running, totals, best = carry
    partial = lax.ppermute(
        jnp.concatenate([running, totals[..., None], best[..., None]], axis=-1),
        "section",
        [(1, 0)],
    )
    other_best = partial[..., head_size + 1]
    merged_best = jnp.maximum(best, other_best)
    own_factor = jnp.exp(best - merged_best)
    other_factor = jnp.exp(other_best - merged_best)
    running = running * own_factor[..., None] + partial[..., :head_size] * other_factor[..., None]
    totals = totals * own_factor + partial[..., head_size] * other_factor
    attention = running / jnp.maximum(totals, 1.0)[..., None]
    attention = attention.transpose(2, 0, 1, 3).reshape(row_count, query_head_rows * head_size)
    attention = jnp.where(valid_rows[:, None], attention, 0.0).astype(jnp.bfloat16)
    projected = jnp.dot(attention, mixing[0], preferred_element_type=jnp.float32)

    members = lax.axis_size("tp")
    member = lax.axis_index("tp")
    width = feature_count // members
    terms = projected.astype(jnp.bfloat16)
    summed = residual.astype(jnp.float32) + lax.dynamic_slice_in_dim(
        terms, member * width, width, 1
    ).astype(jnp.float32)
    for step in range(1, members):
        target = (member + step) % members
        sent = lax.dynamic_slice_in_dim(terms, target * width, width, 1)
        pairs = [(m, (m + step) % members) for m in range(members)]
        summed = summed + lax.ppermute(sent, ("section", "tp"), pairs).astype(jnp.float32)
    own_hidden = summed.astype(jnp.bfloat16)
    arrived = jnp.stack(
        [
            lax.ppermute(
                own_hidden,
                ("section", "tp"),
                [(m, members + (m + step) % members) for m in range(members)],
            )
            for step in range(members)
        ],
        0,
    )
    local_activations = jnp.where(section_index == 0, own_hidden, arrived[0])

    masked_keys = jnp.where(valid_rows[:, None], own_keys, jnp.zeros_like(own_keys)).reshape(
        row_count, key_heads, head_size
    )
    wide_keys = masked_keys.astype(jnp.float32)
    decays = log_decay * valid_rows[:, None].astype(jnp.float32)
    wide = arrived.astype(jnp.float32)
    inverse_scale = lax.rsqrt(
        jnp.sum(wide * wide, axis=(0, 2))[:, None] / feature_count + 1e-05
    )
    payload_sum = jnp.zeros((row_count, mixing.shape[1]), jnp.float32)
    for step in range(members):
        owner = (member - step) % members
        gain = lax.dynamic_slice_in_dim(norm_gain, owner * width, width, 0).astype(jnp.float32)
        normed = (wide[step] * inverse_scale * gain).astype(jnp.bfloat16)
        payload_sum = payload_sum + lax.dot_general(
            normed,
            lax.dynamic_slice_in_dim(mixing[0], owner * width, width, 1),
            (((1,), (1,)), ((), ())),
            preferred_element_type=jnp.float32,
        )
    payload_vectors = payload_sum.astype(jnp.bfloat16)
    cumulated = jnp.cumsum(decays, axis=0).reshape(row_count, key_heads, group_size)
    value_rows = payload_vectors.astype(jnp.float32).reshape(
        row_count, key_heads, group_size, head_size
    )
    fresh_state = jnp.einsum(
        "sgd,sgje->gdje",
        wide_keys,
        value_rows * jnp.exp(cumulated[-1] - cumulated)[..., None],
        precision=lax.Precision.HIGHEST,
    )

    def chain(previous_entry, latter):
        latter_total = latter[:, :1]
        return jnp.concatenate(
            [
                previous_entry[:, :1] + latter_total,
                previous_entry[:, 1:] * jnp.exp(latter_total) + latter[:, 1:],
            ],
            axis=1,
        )

    def sent_along(entry, by):
        total = entry[:, :1]
        high = total.astype(jnp.bfloat16)
        low = (total - high.astype(jnp.float32)).astype(jnp.bfloat16)
        narrow = jnp.concatenate([high, low, entry[:, 1:].astype(jnp.bfloat16)], axis=1)
        moved = passed_along(narrow, by, 1).astype(jnp.float32)
        return jnp.concatenate([moved[:, :1] + moved[:, 1:2], moved[:, 2:]], axis=1)

    total_rows = jnp.broadcast_to(cumulated[-1][:, None, :, None], (key_heads, 1, group_size, head_size))
    own_entry = jnp.concatenate([total_rows, fresh_state], axis=1)
    entry = sent_along(own_entry, 1)
    for times in range(2, 4):
        entry = chain(sent_along(own_entry, times), entry)
    reach = 3
    while reach < shards:
        spread = 4 if reach < 12 else -(-shards // reach)
        joined = entry
        for times in range(1, spread):
            joined = chain(sent_along(entry, times * reach), joined)
        entry = joined
        reach *= spread
    incoming = entry[:, 1:]

    query_narrow = queries[0].reshape(row_count, key_heads, group_size, head_size)
    query_wide = query_narrow.astype(jnp.float32)
    products = jnp.einsum(
        "rgjd,sgd->gjrs", query_narrow, masked_keys, preferred_element_type=jnp.float32
    )
    ordered = cumulated.transpose(1, 2, 0)
    spread = ordered[..., :, None] - ordered[..., None, :]
    triangle = positions[:, None] >= positions[None, :]
    damping = jnp.where(triangle, jnp.exp(jnp.minimum(spread, 0.0)), 0.0)
    intra = jnp.einsum(
        "gjrs,sgje->rgje", products * damping, value_rows, precision=lax.Precision.HIGHEST
    )
    inter = (
        jnp.einsum("rgjd,gdje->rgje", query_wide, incoming, precision=lax.Precision.HIGHEST)
        * jnp.exp(cumulated)[..., None]
    )
    mixed = (inter + intra).reshape(row_count, query_head_rows, head_size)
    scaled = mixed * lax.rsqrt(jnp.mean(mixed * mixed, axis=-1, keepdims=True) + 1e-05)
    gating = spike_counts.astype(jnp.float32).reshape(
        row_count, query_head_rows, head_size
    ) * thresholds.reshape(query_head_rows, head_size)
    gated = jnp.where(
        valid_rows[:, None],
        (scaled * gating).reshape(row_count, query_head_rows * head_size),
        0.0,
    ).astype(jnp.bfloat16)
    head_outputs = jnp.where(section_index == 0, attention, gated)[None]
    return (head_outputs, local_activations)


def solution(mesh):
    return jax.shard_map(
        body,
        mesh=mesh,
        in_specs=(
            P("ctx", "tp"),
            P("section", "ctx", "tp"),
            P("section", "ctx", "tp"),
            P("ctx", "tp"),
            P("section", "tp", None),
            P(),
            P("ctx", "tp"),
            P("ctx", "tp"),
            P("tp"),
            P(),
        ),
        out_specs=(P("section", "ctx", "tp"), P("ctx", "tp")),
        check_vma=False,
    )
```

```python
import math

import jax
import jax.numpy as jnp
from jax import lax
from jax.sharding import PartitionSpec as P

HEAD = 128
WINDOW = 4096


def passed_along(x, by, section):
    shards = lax.axis_size("ctx")
    sections = lax.axis_size("section")
    pairs = [
        (i * sections + section, (i + by) * sections + section)
        for i in range(shards)
        if 0 <= i + by < shards
    ]
    return lax.ppermute(x, ("ctx", "section"), pairs)


def body(
    residual,
    queries,
    keys,
    window_values,
    mixing,
    norm_gain,
    log_decay,
    spike_counts,
    thresholds,
    lengths,
):
    section_index = lax.axis_index("section")
    shard_index = lax.axis_index("ctx")
    shards = lax.axis_size("ctx")
    row_count = keys.shape[1]
    head_size = HEAD
    key_heads = keys.shape[2] // head_size
    query_head_rows = queries.shape[2] // head_size
    group_size = query_head_rows // key_heads
    span_blocks = WINDOW // row_count
    feature_count = mixing.shape[2]
    scale = 1.0 / math.sqrt(head_size)
    positions = jnp.arange(row_count, dtype=jnp.int32)
    valid_rows = positions < lengths[shard_index]
    own_keys = keys[0]

    key_width = own_keys.shape[1]
    query_width = queries.shape[2]
    mate_copy = lax.ppermute(
        jnp.concatenate([queries[0], own_keys], axis=1), "section", [(0, 1)]
    )
    first_queries = jnp.where(section_index == 0, queries[0], mate_copy[:, :query_width])
    first_keys = jnp.where(section_index == 0, own_keys, mate_copy[:, query_width:])
    query_rows = first_queries.reshape(row_count, key_heads, group_size, head_size)
    base_distance = positions[:, None] - positions[None, :]
    packed = jnp.concatenate([first_keys, window_values], axis=1)
    sections = lax.axis_size("section")
    relay = 12
    bundled = (span_blocks - relay) // 2 + 1
    plan = [(0, 1), (2, 3), (4, 9), (6, 11), (8, None), (10, None)]
    running = jnp.zeros((key_heads, group_size, row_count, head_size), jnp.float32)
    totals = jnp.zeros((key_heads, group_size, row_count), jnp.float32)
    best = jnp.full((key_heads, group_size, row_count), -1e30, jnp.float32)

    def blend(carry, joined, distance_blocks):
        running, totals, best = carry
        key_block, value_block = joined[:, :key_width], joined[:, key_width:]
        source = shard_index - distance_blocks
        key_valid = (source >= 0) & (positions < lengths[jnp.clip(source, 0, shards - 1)])
        scores = (
            jnp.einsum(
                "rgjd,kgd->gjrk",
                query_rows,
                key_block.reshape(row_count, key_heads, head_size),
                preferred_element_type=jnp.float32,
            )
            * scale
        )
        distance = base_distance + distance_blocks * row_count
        allowed = key_valid[None, :] & (distance >= 0) & (distance < WINDOW)
        scores = jnp.where(allowed, scores, -1e30)
        new_best = jnp.maximum(best, jnp.max(scores, axis=-1))
        factor = jnp.exp(best - new_best)
        weights = jnp.where(allowed, jnp.exp(scores - new_best[..., None]), 0.0)
        blended = jnp.einsum(
            "gjrk,kgd->gjrd",
            weights.astype(jnp.bfloat16),
            value_block.reshape(row_count, key_heads, head_size),
            preferred_element_type=jnp.float32,
        )
        return (
            running * factor[..., None] + blended,
            totals * factor + jnp.sum(weights, axis=-1),
            new_best,
        )

    def both_pairs(first_distance, second_distance):
        pairs = []
        for taken, owner in ((first_distance, 0), (second_distance, 1)):
            if taken:
                pairs += [
                    (i * sections + owner, (i + taken) * sections + owner)
                    for i in range(shards)
                    if i + taken < shards
                ]
        return pairs

    carry = (running, totals, best)
    held = []
    for first_distance, second_distance in plan:
        joined = lax.ppermute(packed, ("ctx", "section"), both_pairs(first_distance, second_distance))
        if first_distance == 0:
            joined = jnp.where(section_index == 0, packed, joined)
        held.append(joined)
        if second_distance is None:
            second_distance = span_blocks + 1
        carry = blend(carry, joined, jnp.where(section_index == 0, first_distance, second_distance))
    bundle = lax.ppermute(
        jnp.concatenate(held[:bundled], axis=1), ("ctx", "section"), both_pairs(relay, relay)
    )
    forwarded = lax.ppermute(
        jnp.concatenate(held[2:4], axis=1),
        ("ctx", "section"),
        [(i * sections, (i + 1) * sections + 1) for i in range(shards - 1)],
    )
    slots = [
        (bundle, 0, forwarded, 0, relay, 5),
        (bundle, 1, forwarded, 1, relay + 2, 7),
        (bundle, 2, bundle, 0, relay + 4, relay + 1),
        (bundle, 2, bundle, 1, span_blocks + 1, relay + 3),
    ]
    width_of = 2 * key_width
    for first_array, first_slot, second_array, second_slot, first_distance, second_distance in slots:
        joined = jnp.where(
            section_index == 0,
            first_array[:, first_slot * width_of:(first_slot + 1) * width_of],
            second_array[:, second_slot * width_of:(second_slot + 1) * width_of],
        )
        carry = blend(carry, joined, jnp.where(section_index == 0, first_distance, second_distance))
    running, totals, best = carry
    partial = lax.ppermute(
        jnp.concatenate([running, totals[..., None], best[..., None]], axis=-1),
        "section",
        [(1, 0)],
    )
    other_best = partial[..., head_size + 1]
    merged_best = jnp.maximum(best, other_best)
    own_factor = jnp.exp(best - merged_best)
    other_factor = jnp.exp(other_best - merged_best)
    running = running * own_factor[..., None] + partial[..., :head_size] * other_factor[..., None]
    totals = totals * own_factor + partial[..., head_size] * other_factor
    attention = running / jnp.maximum(totals, 1.0)[..., None]
    attention = attention.transpose(2, 0, 1, 3).reshape(row_count, query_head_rows * head_size)
    attention = jnp.where(valid_rows[:, None], attention, 0.0).astype(jnp.bfloat16)
    projected = jnp.dot(attention, mixing[0], preferred_element_type=jnp.float32)

    members = lax.axis_size("tp")
    member = lax.axis_index("tp")
    width = feature_count // members
    terms = projected.astype(jnp.bfloat16)
    summed = residual.astype(jnp.float32) + lax.dynamic_slice_in_dim(
        terms, member * width, width, 1
    ).astype(jnp.float32)
    for step in range(1, members):
        target = (member + step) % members
        sent = lax.dynamic_slice_in_dim(terms, target * width, width, 1)
        pairs = [(m, (m + step) % members) for m in range(members)]
        summed = summed + lax.ppermute(sent, ("section", "tp"), pairs).astype(jnp.float32)
    own_hidden = summed.astype(jnp.bfloat16)
    arrived = jnp.stack(
        [
            lax.ppermute(
                own_hidden,
                ("section", "tp"),
                [(m, members + (m + step) % members) for m in range(members)],
            )
            for step in range(members)
        ],
        0,
    )
    local_activations = jnp.where(section_index == 0, own_hidden, arrived[0])

    masked_keys = jnp.where(valid_rows[:, None], own_keys, jnp.zeros_like(own_keys)).reshape(
        row_count, key_heads, head_size
    )
    wide_keys = masked_keys.astype(jnp.float32)
    decays = log_decay * valid_rows[:, None].astype(jnp.float32)
    wide = arrived.astype(jnp.float32)
    inverse_scale = lax.rsqrt(
        jnp.sum(wide * wide, axis=(0, 2))[:, None] / feature_count + 1e-05
    )
    payload_sum = jnp.zeros((row_count, mixing.shape[1]), jnp.float32)
    for step in range(members):
        owner = (member - step) % members
        gain = lax.dynamic_slice_in_dim(norm_gain, owner * width, width, 0).astype(jnp.float32)
        normed = (wide[step] * inverse_scale * gain).astype(jnp.bfloat16)
        payload_sum = payload_sum + lax.dot_general(
            normed,
            lax.dynamic_slice_in_dim(mixing[0], owner * width, width, 1),
            (((1,), (1,)), ((), ())),
            preferred_element_type=jnp.float32,
        )
    payload_vectors = payload_sum.astype(jnp.bfloat16)
    cumulated = jnp.cumsum(decays, axis=0).reshape(row_count, key_heads, group_size)
    value_rows = payload_vectors.astype(jnp.float32).reshape(
        row_count, key_heads, group_size, head_size
    )
    fresh_state = jnp.einsum(
        "sgd,sgje->gdje",
        wide_keys,
        value_rows * jnp.exp(cumulated[-1] - cumulated)[..., None],
        precision=lax.Precision.HIGHEST,
    )

    def chain(previous_entry, latter):
        latter_total = latter[:, :1]
        return jnp.concatenate(
            [
                previous_entry[:, :1] + latter_total,
                previous_entry[:, 1:] * jnp.exp(latter_total) + latter[:, 1:],
            ],
            axis=1,
        )

    def sent_along(entry, by):
        total = entry[:, :1]
        high = total.astype(jnp.bfloat16)
        low = (total - high.astype(jnp.float32)).astype(jnp.bfloat16)
        narrow = jnp.concatenate([high, low, entry[:, 1:].astype(jnp.bfloat16)], axis=1)
        moved = passed_along(narrow, by, 1).astype(jnp.float32)
        return jnp.concatenate([moved[:, :1] + moved[:, 1:2], moved[:, 2:]], axis=1)

    total_rows = jnp.broadcast_to(cumulated[-1][:, None, :, None], (key_heads, 1, group_size, head_size))
    own_entry = jnp.concatenate([total_rows, fresh_state], axis=1)
    entry = sent_along(own_entry, 1)
    for times in range(2, 5):
        entry = chain(sent_along(own_entry, times), entry)
    reach = 4
    while reach < shards:
        spread = 3 if reach < 12 else -(-shards // reach)
        joined = entry
        for times in range(1, spread):
            joined = chain(sent_along(entry, times * reach), joined)
        entry = joined
        reach *= spread
    incoming = entry[:, 1:]

    query_narrow = queries[0].reshape(row_count, key_heads, group_size, head_size)
    query_wide = query_narrow.astype(jnp.float32)
    products = jnp.einsum(
        "rgjd,sgd->gjrs", query_narrow, masked_keys, preferred_element_type=jnp.float32
    )
    ordered = cumulated.transpose(1, 2, 0)
    spread = ordered[..., :, None] - ordered[..., None, :]
    triangle = positions[:, None] >= positions[None, :]
    damping = jnp.where(triangle, jnp.exp(jnp.minimum(spread, 0.0)), 0.0)
    intra = jnp.einsum(
        "gjrs,sgje->rgje", products * damping, value_rows, precision=lax.Precision.HIGHEST
    )
    inter = (
        jnp.einsum("rgjd,gdje->rgje", query_wide, incoming, precision=lax.Precision.HIGHEST)
        * jnp.exp(cumulated)[..., None]
    )
    mixed = (inter + intra).reshape(row_count, query_head_rows, head_size)
    scaled = mixed * lax.rsqrt(jnp.mean(mixed * mixed, axis=-1, keepdims=True) + 1e-05)
    gating = spike_counts.astype(jnp.float32).reshape(
        row_count, query_head_rows, head_size
    ) * thresholds.reshape(query_head_rows, head_size)
    gated = jnp.where(
        valid_rows[:, None],
        (scaled * gating).reshape(row_count, query_head_rows * head_size),
        0.0,
    ).astype(jnp.bfloat16)
    head_outputs = jnp.where(section_index == 0, attention, gated)[None]
    return (head_outputs, local_activations)


def solution(mesh):
    return jax.shard_map(
        body,
        mesh=mesh,
        in_specs=(
            P("ctx", "tp"),
            P("section", "ctx", "tp"),
            P("section", "ctx", "tp"),
            P("ctx", "tp"),
            P("section", "tp", None),
            P(),
            P("ctx", "tp"),
            P("ctx", "tp"),
            P("tp"),
            P(),
        ),
        out_specs=(P("section", "ctx", "tp"), P("ctx", "tp")),
        check_vma=False,
    )
```

```python
import math

import jax
import jax.numpy as jnp
from jax import lax
from jax.sharding import PartitionSpec as P

HEAD = 128
WINDOW = 4096


def passed_along(x, by, section):
    shards = lax.axis_size("ctx")
    sections = lax.axis_size("section")
    pairs = [
        (i * sections + section, (i + by) * sections + section)
        for i in range(shards)
        if 0 <= i + by < shards
    ]
    return lax.ppermute(x, ("ctx", "section"), pairs)


def body(
    residual,
    queries,
    keys,
    window_values,
    mixing,
    norm_gain,
    log_decay,
    spike_counts,
    thresholds,
    lengths,
):
    section_index = lax.axis_index("section")
    shard_index = lax.axis_index("ctx")
    shards = lax.axis_size("ctx")
    row_count = keys.shape[1]
    head_size = HEAD
    key_heads = keys.shape[2] // head_size
    query_head_rows = queries.shape[2] // head_size
    group_size = query_head_rows // key_heads
    span_blocks = WINDOW // row_count
    feature_count = mixing.shape[2]
    scale = 1.0 / math.sqrt(head_size)
    positions = jnp.arange(row_count, dtype=jnp.int32)
    valid_rows = positions < lengths[shard_index]
    own_keys = keys[0]

    key_width = own_keys.shape[1]
    query_width = queries.shape[2]
    mate_copy = lax.ppermute(
        jnp.concatenate([queries[0], own_keys], axis=1), "section", [(0, 1)]
    )
    first_queries = jnp.where(section_index == 0, queries[0], mate_copy[:, :query_width])
    first_keys = jnp.where(section_index == 0, own_keys, mate_copy[:, query_width:])
    query_rows = first_queries.reshape(row_count, key_heads, group_size, head_size)
    base_distance = positions[:, None] - positions[None, :]
    packed = jnp.concatenate([first_keys, window_values], axis=1)
    sections = lax.axis_size("section")
    relay = 12
    bundled = (span_blocks - relay) // 2 + 1
    plan = [(0, 1), (2, 3), (4, 9), (6, 11), (8, None)]
    running = jnp.zeros((key_heads, group_size, row_count, head_size), jnp.float32)
    totals = jnp.zeros((key_heads, group_size, row_count), jnp.float32)
    best = jnp.full((key_heads, group_size, row_count), -1e30, jnp.float32)

    def blend(carry, joined, distance_blocks):
        running, totals, best = carry
        key_block, value_block = joined[:, :key_width], joined[:, key_width:]
        source = shard_index - distance_blocks
        key_valid = (source >= 0) & (positions < lengths[jnp.clip(source, 0, shards - 1)])
        scores = (
            jnp.einsum(
                "rgjd,kgd->gjrk",
                query_rows,
                key_block.reshape(row_count, key_heads, head_size),
                preferred_element_type=jnp.float32,
            )
            * scale
        )
        distance = base_distance + distance_blocks * row_count
        allowed = key_valid[None, :] & (distance >= 0) & (distance < WINDOW)
        scores = jnp.where(allowed, scores, -1e30)
        new_best = jnp.maximum(best, jnp.max(scores, axis=-1))
        factor = jnp.exp(best - new_best)
        weights = jnp.where(allowed, jnp.exp(scores - new_best[..., None]), 0.0)
        blended = jnp.einsum(
            "gjrk,kgd->gjrd",
            weights.astype(jnp.bfloat16),
            value_block.reshape(row_count, key_heads, head_size),
            preferred_element_type=jnp.float32,
        )
        return (
            running * factor[..., None] + blended,
            totals * factor + jnp.sum(weights, axis=-1),
            new_best,
        )

    def both_pairs(first_distance, second_distance):
        pairs = []
        for taken, owner in ((first_distance, 0), (second_distance, 1)):
            if taken:
                pairs += [
                    (i * sections + owner, (i + taken) * sections + owner)
                    for i in range(shards)
                    if i + taken < shards
                ]
        return pairs

    carry = (running, totals, best)
    held = []
    for first_distance, second_distance in plan:
        joined = lax.ppermute(packed, ("ctx", "section"), both_pairs(first_distance, second_distance))
        if first_distance == 0:
            joined = jnp.where(section_index == 0, packed, joined)
        held.append(joined)
        if second_distance is None:
            second_distance = span_blocks + 1
        carry = blend(carry, joined, jnp.where(section_index == 0, first_distance, second_distance))
    bundle = lax.ppermute(
        jnp.concatenate(held[:bundled], axis=1), ("ctx", "section"), both_pairs(relay, relay)
    )
    forwarded = lax.ppermute(
        jnp.concatenate(held[2:4], axis=1),
        ("ctx", "section"),
        [(i * sections, (i + 1) * sections + 1) for i in range(shards - 1)],
    )
    returned = lax.ppermute(
        held[2],
        ("ctx", "section"),
        [(i * sections + 1, (i + 1) * sections) for i in range(shards - 1)],
    )
    slots = [
        (bundle, 0, forwarded, 0, relay, 5),
        (bundle, 1, forwarded, 1, relay + 2, 7),
        (bundle, 2, bundle, 0, relay + 4, relay + 1),
        (returned, 0, bundle, 1, 10, relay + 3),
    ]
    width_of = 2 * key_width
    for first_array, first_slot, second_array, second_slot, first_distance, second_distance in slots:
        joined = jnp.where(
            section_index == 0,
            first_array[:, first_slot * width_of:(first_slot + 1) * width_of],
            second_array[:, second_slot * width_of:(second_slot + 1) * width_of],
        )
        carry = blend(carry, joined, jnp.where(section_index == 0, first_distance, second_distance))
    running, totals, best = carry
    partial = lax.ppermute(
        jnp.concatenate([running, totals[..., None], best[..., None]], axis=-1),
        "section",
        [(1, 0)],
    )
    other_best = partial[..., head_size + 1]
    merged_best = jnp.maximum(best, other_best)
    own_factor = jnp.exp(best - merged_best)
    other_factor = jnp.exp(other_best - merged_best)
    running = running * own_factor[..., None] + partial[..., :head_size] * other_factor[..., None]
    totals = totals * own_factor + partial[..., head_size] * other_factor
    attention = running / jnp.maximum(totals, 1.0)[..., None]
    attention = attention.transpose(2, 0, 1, 3).reshape(row_count, query_head_rows * head_size)
    attention = jnp.where(valid_rows[:, None], attention, 0.0).astype(jnp.bfloat16)
    projected = jnp.dot(attention, mixing[0], preferred_element_type=jnp.float32)

    members = lax.axis_size("tp")
    member = lax.axis_index("tp")
    width = feature_count // members
    terms = projected.astype(jnp.bfloat16)
    summed = residual.astype(jnp.float32) + lax.dynamic_slice_in_dim(
        terms, member * width, width, 1
    ).astype(jnp.float32)
    for step in range(1, members):
        target = (member + step) % members
        sent = lax.dynamic_slice_in_dim(terms, target * width, width, 1)
        pairs = [(m, (m + step) % members) for m in range(members)]
        summed = summed + lax.ppermute(sent, ("section", "tp"), pairs).astype(jnp.float32)
    own_hidden = summed.astype(jnp.bfloat16)
    arrived = jnp.stack(
        [
            lax.ppermute(
                own_hidden,
                ("section", "tp"),
                [(m, members + (m + step) % members) for m in range(members)],
            )
            for step in range(members)
        ],
        0,
    )
    local_activations = jnp.where(section_index == 0, own_hidden, arrived[0])

    masked_keys = jnp.where(valid_rows[:, None], own_keys, jnp.zeros_like(own_keys)).reshape(
        row_count, key_heads, head_size
    )
    wide_keys = masked_keys.astype(jnp.float32)
    decays = log_decay * valid_rows[:, None].astype(jnp.float32)
    wide = arrived.astype(jnp.float32)
    inverse_scale = lax.rsqrt(
        jnp.sum(wide * wide, axis=(0, 2))[:, None] / feature_count + 1e-05
    )
    payload_sum = jnp.zeros((row_count, mixing.shape[1]), jnp.float32)
    for step in range(members):
        owner = (member - step) % members
        gain = lax.dynamic_slice_in_dim(norm_gain, owner * width, width, 0).astype(jnp.float32)
        normed = (wide[step] * inverse_scale * gain).astype(jnp.bfloat16)
        payload_sum = payload_sum + lax.dot_general(
            normed,
            lax.dynamic_slice_in_dim(mixing[0], owner * width, width, 1),
            (((1,), (1,)), ((), ())),
            preferred_element_type=jnp.float32,
        )
    payload_vectors = payload_sum.astype(jnp.bfloat16)
    cumulated = jnp.cumsum(decays, axis=0).reshape(row_count, key_heads, group_size)
    value_rows = payload_vectors.astype(jnp.float32).reshape(
        row_count, key_heads, group_size, head_size
    )
    fresh_state = jnp.einsum(
        "sgd,sgje->gdje",
        wide_keys,
        value_rows * jnp.exp(cumulated[-1] - cumulated)[..., None],
        precision=lax.Precision.HIGHEST,
    )

    def chain(previous_entry, latter):
        latter_total = latter[:, :1]
        return jnp.concatenate(
            [
                previous_entry[:, :1] + latter_total,
                previous_entry[:, 1:] * jnp.exp(latter_total) + latter[:, 1:],
            ],
            axis=1,
        )

    def sent_along(entry, by):
        total = entry[:, :1]
        high = total.astype(jnp.bfloat16)
        low = (total - high.astype(jnp.float32)).astype(jnp.bfloat16)
        narrow = jnp.concatenate([high, low, entry[:, 1:].astype(jnp.bfloat16)], axis=1)
        moved = passed_along(narrow, by, 1).astype(jnp.float32)
        return jnp.concatenate([moved[:, :1] + moved[:, 1:2], moved[:, 2:]], axis=1)

    total_rows = jnp.broadcast_to(cumulated[-1][:, None, :, None], (key_heads, 1, group_size, head_size))
    own_entry = jnp.concatenate([total_rows, fresh_state], axis=1)
    entry = sent_along(own_entry, 1)
    for times in range(2, 4):
        entry = chain(sent_along(own_entry, times), entry)
    reach = 3
    while reach < shards:
        spread = 4 if reach < 12 else -(-shards // reach)
        joined = entry
        for times in range(1, spread):
            joined = chain(sent_along(entry, times * reach), joined)
        entry = joined
        reach *= spread
    incoming = entry[:, 1:]

    query_narrow = queries[0].reshape(row_count, key_heads, group_size, head_size)
    query_wide = query_narrow.astype(jnp.float32)
    products = jnp.einsum(
        "rgjd,sgd->gjrs", query_narrow, masked_keys, preferred_element_type=jnp.float32
    )
    ordered = cumulated.transpose(1, 2, 0)
    spread = ordered[..., :, None] - ordered[..., None, :]
    triangle = positions[:, None] >= positions[None, :]
    damping = jnp.where(triangle, jnp.exp(jnp.minimum(spread, 0.0)), 0.0)
    intra = jnp.einsum(
        "gjrs,sgje->rgje", products * damping, value_rows, precision=lax.Precision.HIGHEST
    )
    inter = (
        jnp.einsum("rgjd,gdje->rgje", query_wide, incoming, precision=lax.Precision.HIGHEST)
        * jnp.exp(cumulated)[..., None]
    )
    mixed = (inter + intra).reshape(row_count, query_head_rows, head_size)
    scaled = mixed * lax.rsqrt(jnp.mean(mixed * mixed, axis=-1, keepdims=True) + 1e-05)
    gating = spike_counts.astype(jnp.float32).reshape(
        row_count, query_head_rows, head_size
    ) * thresholds.reshape(query_head_rows, head_size)
    gated = jnp.where(
        valid_rows[:, None],
        (scaled * gating).reshape(row_count, query_head_rows * head_size),
        0.0,
    ).astype(jnp.bfloat16)
    head_outputs = jnp.where(section_index == 0, attention, gated)[None]
    return (head_outputs, local_activations)


def solution(mesh):
    return jax.shard_map(
        body,
        mesh=mesh,
        in_specs=(
            P("ctx", "tp"),
            P("section", "ctx", "tp"),
            P("section", "ctx", "tp"),
            P("ctx", "tp"),
            P("section", "tp", None),
            P(),
            P("ctx", "tp"),
            P("ctx", "tp"),
            P("tp"),
            P(),
        ),
        out_specs=(P("section", "ctx", "tp"), P("ctx", "tp")),
        check_vma=False,
    )
```
